32 devices in a mesh: groups: 1, rows: 32 (over z, y, x, core).
Axes of the slice: x: 2, y: 2, z: 4, core: 2. Of those that a mesh axis runs over, the one named last changes fastest.
Arguments:
- acts: bfloat16 [4096, 2, 4096], P(('groups', 'rows')), may hold values from -6 to 6
- grads_out: bfloat16 [4096, 2, 4096], P(('groups', 'rows')), may hold values from -6 to 6
- lengths: int32 [32], P('groups'), may hold values from 1 to 512, 4096 in all
- valid: int32 [4096], P(('groups', 'rows')), may hold values 0 or 1
- proj_in: bfloat16 [4096, 128], replicated, may hold values from -0.09375 to 0.09375
- proj_out: bfloat16 [4096, 128], replicated, may hold values from -0.09375 to 0.09375
- fisher_inv: float32 [2, 4096, 4096], P(None, 'rows'), may hold values from -1 to 2, as said below
- database: float32 [4096, 2, 4096], P(('groups', 'rows')), may hold values from -250 to 250
Outputs:
- zscores: float32 [32, 4096], P(None, ('groups', 'rows'))
The draws below stay inside these ranges and needn't reach their ends.
Inputs may be any that keep to these rules, and one draw needn't show every extreme that they name: The lengths sum to 4096; the largest is exactly 512. `fisher_inv`: each of the 2 blocks is symmetric.
All inputs are finite; a program needn't handle non-finite values. No bound on the sum of `valid` on one device may be relied on, other than what follows from the above.
Results may differ from the reference program's by a relative error of at most 0.0042.
Values sent between devices are 32-bit elements; how exact they have to be, the bound alone decides.
No kernel may reach another device: no remote copies, remote signals or barrier semaphores. Data moves between devices by JAX's collectives and lax.ppermute only.
A program may use at most 64 MiB of HBM per device.

```python
import math
import jax
import jax.numpy as jnp
import numpy as np
from jax import lax

D = 4096
R = 64
KK = 4096
MODS = 2
NQ = 32
TOKENS = 4096
NDB = 4096


def draw_fisher_inv(key, part):
    first_key, second_key = jax.random.split(jax.random.fold_in(key, 11))
    diagonal = jax.random.uniform(first_key, (MODS, KK), jnp.float32, 0.5, 1.5)
    bound = 0.3 / math.sqrt(KK)
    offdiag = jax.random.uniform(second_key, (MODS, KK, KK), jnp.float32, -bound, bound)
    symmetric = offdiag + jnp.swapaxes(offdiag, 1, 2)
    identity = jnp.eye(KK, dtype=jnp.float32)
    return symmetric * (1.0 - identity)[None] + identity[None] * diagonal[:, :, None]


def draw_database(key, part):
    noise_key, common_key = jax.random.split(jax.random.fold_in(key, 23))
    ramp = jnp.arange(NDB, dtype=jnp.float32) / max(NDB - 1, 1)
    noise = jax.random.truncated_normal(noise_key, -6.0, 6.0, (NDB, MODS, KK), jnp.float32)
    common = 0.3 * jax.random.truncated_normal(common_key, -6.0, 6.0, (MODS, KK), jnp.float32)
    scale = jnp.exp(math.log(10.0) * ramp)
    return (noise + common[None]) * scale[:, None, None]


def place_ends(values, stream_key, least, largest):
    dims = values.shape
    index_at = [jax.random.randint(jax.random.fold_in(stream_key, axis), (), 0, dims[axis]) for axis in range(len(dims))]
    values = values.at[tuple(index_at)].set(least)
    longest = dims.index(max(dims))
    index_at[longest] = (index_at[longest] + 1) % dims[longest]
    return values.at[tuple(index_at)].set(largest)


def shard_levels(own_key, dims, pieces, least, top_value):
    gain = 1.0
    for dim, shards_of in pieces:
        heights = jax.random.uniform(jax.random.fold_in(jax.random.fold_in(own_key, 6), dim), (shards_of,), jnp.float32, least / len(pieces), top_value / len(pieces))
        gain = gain * jnp.repeat(jnp.exp(heights), dims[dim] // shards_of).reshape((-1,) + (1,) * (len(dims) - 1 - dim))
    return gain


def profile(amount, total, limit, skew):
    weights = [(1 << 20) // math.isqrt(rank ** skew) + 1 for rank in range(2, amount + 1)]
    spare, holding = total - limit - (amount - 1), [1] * (amount - 1)
    while spare > 0:
        candidates = [i for i in range(amount - 1) if holding[i] < limit]
        mass, budget = sum([weights[i] for i in candidates]), spare
        for i in candidates:
            extra = min(limit - holding[i], max(1, budget * weights[i] // mass), spare)
            holding[i] = holding[i] + extra
            spare = spare - extra
    return np.array([limit] + holding)


def uneven(own_key, amount, total, limit, skew):
    if amount == 2:
        one = jax.random.randint(own_key, (), max(1, total - limit), min(limit, total - 1) + 1)
        return jnp.stack([one, total - one])
    sizes = jnp.asarray(profile(amount, total, limit, skew), jnp.int32)
    couples = (amount - 1) // 2
    giver, receiver = sizes[1:1 + 2 * couples:2], sizes[2:2 + 2 * couples:2]
    room = jnp.minimum(giver - 1, limit - receiver)
    shifted = jax.random.randint(jax.random.fold_in(own_key, 1), (couples,), 0, 1 << 20) % (room + 1)
    sizes = sizes.at[1:1 + 2 * couples:2].set(giver - shifted).at[2:2 + 2 * couples:2].set(receiver + shifted)
    return sizes[jax.random.permutation(jax.random.fold_in(own_key, 2), amount)]


def gaussian(stream_key, extent, width, most, pieces=(), held_as=jnp.bfloat16):
    factor_of = shard_levels(stream_key, extent, pieces, -0.22, 0.18) if pieces else 1.0
    drawn = jax.random.normal(stream_key, extent, jnp.float32) * width * factor_of
    return jnp.minimum(jnp.maximum(drawn, -most), most).astype(held_as)


def setup_inputs(seed: int = 0, part: int = 0) -> dict:
    seeds = jax.random.split(jax.random.key(seed), 9)
    part_keys = jax.random.split(jax.random.fold_in(seeds[8], part), 9)
    return {
        "acts": gaussian(part_keys[0], (TOKENS, MODS, D), 1.0, 6.0, ((0, 32),)),
        "grads_out": gaussian(part_keys[1], (TOKENS, MODS, D), 1.0, 6.0, ((0, 32),)),
        "lengths": uneven(part_keys[2], NQ, TOKENS, TOKENS // 8, 2).astype(jnp.int32),
        "valid": place_ends((jax.random.randint(part_keys[3], (TOKENS,), 0, 4) < 3).astype(jnp.int32), jax.random.fold_in(part_keys[3], 1), 0, 1),
        "proj_in": gaussian(seeds[4], (D, MODS * R), D ** -0.5, 0.09375),
        "proj_out": gaussian(seeds[5], (D, MODS * R), D ** -0.5, 0.09375),
        "fisher_inv": draw_fisher_inv(jax.random.fold_in(seeds[8], 71), part),
        "database": draw_database(jax.random.fold_in(jax.random.fold_in(seeds[8], part), 71), part),
    }


def reference(acts, grads_out, lengths, valid, proj_in, proj_out, fisher_inv, database):
    positions = jnp.arange(TOKENS, dtype=jnp.int32)
    seg_ends = jnp.cumsum(lengths).astype(jnp.int32)
    segment = lax.optimization_barrier(jnp.sum((seg_ends[None, :] <= positions[:, None]).astype(jnp.int32), axis=1))
    selector = ((segment[:, None] == jnp.arange(NQ, dtype=jnp.int32)[None, :]) & (valid[:, None] == 1)).astype(jnp.bfloat16)
    module_sums = []
    for m in range(MODS):
        act_proj = jnp.dot(acts[:, m, :], proj_in[:, m * R:(m + 1) * R], preferred_element_type=jnp.float32).astype(jnp.bfloat16)
        grad_proj = jnp.dot(grads_out[:, m, :], proj_out[:, m * R:(m + 1) * R], preferred_element_type=jnp.float32).astype(jnp.bfloat16)
        spread = (selector[:, :, None] * grad_proj[:, None, :]).reshape(TOKENS, NQ * R)
        module_sum = jnp.dot(spread.T, act_proj, preferred_element_type=jnp.float32)
        module_sums.append(module_sum.reshape(NQ, KK))
    grads = jnp.stack(module_sums, axis=1)
    precond = jnp.stack([jnp.dot(grads[:, m, :], fisher_inv[m], precision=lax.Precision.HIGHEST) for m in range(MODS)], axis=1)
    scores = jnp.einsum('qmk,nmk->qn', precond, database, precision=lax.Precision.HIGHEST)
    avg_score = lax.optimization_barrier(jnp.sum(scores, axis=1)) / NDB
    centred = scores - avg_score[:, None]
    variance = lax.optimization_barrier(jnp.sum(centred * centred, axis=1)) / NDB
    return centred * lax.rsqrt(variance + 1e-06)[:, None]
```

```python
import jax
import jax.numpy as jnp
from jax import lax
from jax.sharding import PartitionSpec as P


def _xor_pairs(size, bit):
    return [(i, i ^ (1 << bit)) for i in range(size)]


def _steps(size):
    steps = size.bit_length() - 1
    assert (1 << steps) == size
    return steps


def _join(mine, other, low, axis):
    return jnp.where(
        low, jnp.concatenate([mine, other], axis), jnp.concatenate([other, mine], axis)
    )


def _allreduce(x, size, axis):
    me = lax.axis_index("rows")
    steps = _steps(size)
    cur = x
    for s in range(steps):
        half = cur.shape[axis] // 2
        lo = lax.slice_in_dim(cur, 0, half, axis=axis)
        hi = lax.slice_in_dim(cur, half, 2 * half, axis=axis)
        low = ((me >> s) & 1) == 0
        keep = jnp.where(low, lo, hi)
        send = jnp.where(low, hi, lo)
        cur = keep + lax.ppermute(send, "rows", _xor_pairs(size, s))
    for s in reversed(range(steps)):
        low = ((me >> s) & 1) == 0
        cur = _join(cur, lax.ppermute(cur, "rows", _xor_pairs(size, s)), low, axis)
    return cur


def _allgather(x, size, axis):
    me = lax.axis_index("rows")
    cur = x
    for s in range(_steps(size)):
        low = ((me >> s) & 1) == 0
        cur = _join(cur, lax.ppermute(cur, "rows", _xor_pairs(size, s)), low, axis)
    return cur


def _butterfly_sum(x, size):
    for s in range(_steps(size)):
        x = x + lax.ppermute(x, "rows", _xor_pairs(size, s))
    return x


def shards(size, acts, grads_out, lengths, valid, proj_in, proj_out, fisher_inv, database):
    tok_rows = acts.shape[0]
    modules = acts.shape[1]
    proj_rank = proj_in.shape[1] // modules
    queries = lengths.shape[0]
    flat_width = proj_rank * proj_rank
    first_pos = lax.axis_index("rows") * tok_rows
    positions = first_pos + jnp.arange(tok_rows, dtype=jnp.int32)
    seg_ends = jnp.cumsum(lengths)
    segment = jnp.sum((seg_ends[None, :] <= positions[:, None]).astype(jnp.int32), axis=1)
    selector = (
        (segment[:, None] == jnp.arange(queries, dtype=jnp.int32)[None, :]) & (valid[:, None] == 1)
    ).astype(jnp.bfloat16)
    module_sums = []
    for m in range(modules):
        act_proj = jnp.dot(
            acts[:, m, :],
            proj_in[:, m * proj_rank : (m + 1) * proj_rank],
            preferred_element_type=jnp.float32,
        ).astype(jnp.bfloat16)
        grad_proj = jnp.dot(
            grads_out[:, m, :],
            proj_out[:, m * proj_rank : (m + 1) * proj_rank],
            preferred_element_type=jnp.float32,
        ).astype(jnp.bfloat16)
        spread = (selector[:, :, None] * grad_proj[:, None, :]).reshape(
            tok_rows, queries * proj_rank
        )
        module_sum = lax.dot_general(
            spread, act_proj, (((0,), (0,)), ((), ())), preferred_element_type=jnp.float32
        )
        module_sums.append(module_sum.reshape(queries, flat_width))
    partial_value = jnp.stack(module_sums, axis=1)
    summed = _allreduce(partial_value, size, 2)
    precond_cols = jnp.einsum("qmk,mck->qmc", summed, fisher_inv, precision=lax.Precision.HIGHEST)
    scores = jnp.einsum(
        "qmk,nmk->qn",
        _allgather(precond_cols, size, 2),
        database,
        precision=lax.Precision.HIGHEST,
    )
    db_count = database.shape[0] * size
    moments = _butterfly_sum(
        jnp.stack([jnp.sum(scores, axis=1), jnp.sum(scores * scores, axis=1)]), size
    )
    avg_score = moments[0] / db_count
    variance = moments[1] / db_count - avg_score * avg_score
    centred = scores - avg_score[:, None]
    return centred * lax.rsqrt(variance + 1e-06)[:, None]


def solution(mesh):
    size = mesh.shape["rows"]
    placed = (
        P(("groups", "rows"), None, None),
        P(("groups", "rows"), None, None),
        P("groups"),
        P(("groups", "rows")),
        P(),
        P(),
        P(None, "rows", None),
        P(("groups", "rows"), None, None),
    )
    return jax.shard_map(
        lambda *a: shards(size, *a),
        mesh=mesh,
        in_specs=placed,
        out_specs=P(None, ("groups", "rows")),
        check_vma=False,
    )
```

```python
import jax
import jax.numpy as jnp
from jax import lax
from jax.sharding import PartitionSpec as P


def _xor_pairs(size, bit):
    return [(i, i ^ (1 << bit)) for i in range(size)]


def _steps(size):
    steps = size.bit_length() - 1
    assert (1 << steps) == size
    return steps


def _join(mine, other, low, axis):
    return jnp.where(
        low, jnp.concatenate([mine, other], axis), jnp.concatenate([other, mine], axis)
    )


def _allreduce(x, size, axis):
    me = lax.axis_index("rows")
    steps = _steps(size)
    cur = x
    for s in range(steps):
        half = cur.shape[axis] // 2
        lo = lax.slice_in_dim(cur, 0, half, axis=axis)
        hi = lax.slice_in_dim(cur, half, 2 * half, axis=axis)
        low = ((me >> s) & 1) == 0
        keep = jnp.where(low, lo, hi)
        send = jnp.where(low, hi, lo)
        cur = keep + lax.ppermute(send, "rows", _xor_pairs(size, s))
    for s in reversed(range(steps)):
        low = ((me >> s) & 1) == 0
        cur = _join(cur, lax.ppermute(cur, "rows", _xor_pairs(size, s)), low, axis)
    return cur


def _allgather(x, size):
    me = lax.axis_index("rows")
    cur = x
    for s in reversed(range(_steps(size))):
        low = ((me >> s) & 1) == 0
        other = lax.ppermute(cur, "rows", _xor_pairs(size, s))
        cur = jnp.where(low, jnp.stack([cur, other], -2), jnp.stack([other, cur], -2))
    return cur.reshape(*x.shape[:-1], size * x.shape[-1])


def _bf16_round(x):
    return lax.reduce_precision(x, exponent_bits=8, mantissa_bits=7)


def _butterfly_sum(x, size):
    for s in range(_steps(size)):
        x = x + lax.ppermute(x, "rows", _xor_pairs(size, s))
    return x


def shards(size, acts, grads_out, lengths, valid, proj_in, proj_out, fisher_inv, database):
    tok_rows = acts.shape[0]
    modules = acts.shape[1]
    proj_rank = proj_in.shape[1] // modules
    queries = lengths.shape[0]
    flat_width = proj_rank * proj_rank
    first_pos = lax.axis_index("rows") * tok_rows
    positions = first_pos + jnp.arange(tok_rows, dtype=jnp.int32)
    seg_ends = jnp.cumsum(lengths)
    segment = jnp.sum((seg_ends[None, :] <= positions[:, None]).astype(jnp.int32), axis=1)
    selector = (
        (segment[:, None] == jnp.arange(queries, dtype=jnp.int32)[None, :]) & (valid[:, None] == 1)
    ).astype(jnp.bfloat16)
    owner = (jnp.arange(modules * proj_rank) // proj_rank)[None, :] == jnp.arange(modules)[:, None]
    w_in = jnp.where(owner[:, None, :], proj_in[None, :, :], jnp.zeros((), proj_in.dtype))
    w_out = jnp.where(owner[:, None, :], proj_out[None, :, :], jnp.zeros((), proj_out.dtype))
    dims = (((1, 2), (0, 1)), ((), ()))
    act_proj = lax.dot_general(acts, w_in, dims, preferred_element_type=jnp.float32)
    grad_proj = lax.dot_general(grads_out, w_out, dims, preferred_element_type=jnp.float32)
    act_proj = _bf16_round(act_proj).reshape(tok_rows, modules, proj_rank)
    grad_proj = _bf16_round(grad_proj).reshape(tok_rows, modules, proj_rank)
    outer = (grad_proj[:, :, :, None] * act_proj[:, :, None, :]).reshape(tok_rows, modules * flat_width)
    high = _bf16_round(outer)
    low = outer - high
    tdims = (((0,), (0,)), ((), ()))
    partial_value = lax.dot_general(
        selector, high.astype(jnp.bfloat16), tdims, preferred_element_type=jnp.float32
    ) + lax.dot_general(selector, low.astype(jnp.bfloat16), tdims, preferred_element_type=jnp.float32)
    partial_value = partial_value.reshape(queries, modules, flat_width)
    summed = _allreduce(partial_value, size, 2)
    precond_cols = jnp.einsum("qmk,mck->qmc", summed, fisher_inv, precision=lax.Precision.HIGH)
    scores = jnp.einsum(
        "qmk,nmk->qn",
        _allgather(precond_cols, size),
        database,
        precision=lax.Precision.HIGH,
    )
    db_count = database.shape[0] * size
    moments = _butterfly_sum(
        jnp.stack([jnp.sum(scores, axis=1), jnp.sum(scores * scores, axis=1)]), size
    )
    avg_score = moments[0] / db_count
    variance = moments[1] / db_count - avg_score * avg_score
    centred = scores - avg_score[:, None]
    return centred * lax.rsqrt(variance + 1e-06)[:, None]


def solution(mesh):
    size = mesh.shape["rows"]
    placed = (
        P(("groups", "rows"), None, None),
        P(("groups", "rows"), None, None),
        P("groups"),
        P(("groups", "rows")),
        P(),
        P(),
        P(None, "rows", None),
        P(("groups", "rows"), None, None),
    )
    return jax.shard_map(
        lambda *a: shards(size, *a),
        mesh=mesh,
        in_specs=placed,
        out_specs=P(None, ("groups", "rows")),
        check_vma=False,
    )
```

```python
import jax
import jax.numpy as jnp
from jax import lax
from jax.experimental import pallas as pl
from jax.sharding import PartitionSpec as P


def _xor_pairs(size, bit):
    return [(i, i ^ (1 << bit)) for i in range(size)]


def _steps(size):
    steps = size.bit_length() - 1
    assert (1 << steps) == size
    return steps


def _join(mine, other, low, axis):
    return jnp.where(
        low, jnp.concatenate([mine, other], axis), jnp.concatenate([other, mine], axis)
    )


def _allreduce(x, size, axis):
    me = lax.axis_index("rows")
    steps = _steps(size)
    cur = x
    for s in range(steps):
        half = cur.shape[axis] // 2
        lo = lax.slice_in_dim(cur, 0, half, axis=axis)
        hi = lax.slice_in_dim(cur, half, 2 * half, axis=axis)
        low = ((me >> s) & 1) == 0
        keep = jnp.where(low, lo, hi)
        send = jnp.where(low, hi, lo)
        cur = keep + lax.ppermute(send, "rows", _xor_pairs(size, s))
    for s in reversed(range(steps)):
        low = ((me >> s) & 1) == 0
        cur = _join(cur, lax.ppermute(cur, "rows", _xor_pairs(size, s)), low, axis)
    return cur


def _allgather(x, size):
    me = lax.axis_index("rows")
    cur = x
    for s in reversed(range(_steps(size))):
        low = ((me >> s) & 1) == 0
        other = lax.ppermute(cur, "rows", _xor_pairs(size, s))
        cur = jnp.where(low, jnp.stack([cur, other], -2), jnp.stack([other, cur], -2))
    return cur.reshape(*x.shape[:-1], size * x.shape[-1])


def _bf16_round(x):
    return lax.reduce_precision(x, exponent_bits=8, mantissa_bits=7)


def _butterfly_sum(x, size):
    for s in range(_steps(size)):
        x = x + lax.ppermute(x, "rows", _xor_pairs(size, s))
    return x


def _sums_kernel(acts_ref, gout_ref, pin_ref, pout_ref, sel_ref, out_ref):
    modules = acts_ref.shape[1]
    rank = pin_ref.shape[1] // modules
    width = rank * rank
    col = lax.broadcasted_iota(jnp.int32, (rank, width), 1)
    row = lax.broadcasted_iota(jnp.int32, (rank, width), 0)
    repeat = (col // rank == row).astype(jnp.bfloat16)
    tile = (col % rank == row).astype(jnp.bfloat16)
    sel = sel_ref[...]
    for m in range(modules):
        cols = slice(m * rank, (m + 1) * rank)
        act_proj = jnp.dot(acts_ref[:, m, :], pin_ref[:, cols], preferred_element_type=jnp.float32)
        grad_proj = jnp.dot(gout_ref[:, m, :], pout_ref[:, cols], preferred_element_type=jnp.float32)
        act_wide = jnp.dot(act_proj.astype(jnp.bfloat16), tile, preferred_element_type=jnp.float32)
        grad_wide = jnp.dot(grad_proj.astype(jnp.bfloat16), repeat, preferred_element_type=jnp.float32)
        outer = grad_wide * act_wide
        high = outer.astype(jnp.bfloat16)
        low = (outer - high.astype(jnp.float32)).astype(jnp.bfloat16)
        out_ref[:, m, :] = jnp.dot(sel, high, preferred_element_type=jnp.float32) + jnp.dot(
            sel, low, preferred_element_type=jnp.float32
        )


def _module_sums(acts, grads_out, proj_in, proj_out, selector_t):
    queries = selector_t.shape[0]
    modules = acts.shape[1]
    rank = proj_in.shape[1] // modules
    return pl.pallas_call(
        _sums_kernel,
        out_shape=jax.ShapeDtypeStruct((queries, modules, rank * rank), jnp.float32),
    )(acts, grads_out, proj_in, proj_out, selector_t)


def shards(size, acts, grads_out, lengths, valid, proj_in, proj_out, fisher_inv, database):
    tok_rows = acts.shape[0]
    modules = acts.shape[1]
    proj_rank = proj_in.shape[1] // modules
    queries = lengths.shape[0]
    flat_width = proj_rank * proj_rank
    first_pos = lax.axis_index("rows") * tok_rows
    positions = first_pos + jnp.arange(tok_rows, dtype=jnp.int32)
    seg_ends = jnp.cumsum(lengths)
    segment = jnp.sum((seg_ends[None, :] <= positions[:, None]).astype(jnp.int32), axis=1)
    selector = (
        (segment[:, None] == jnp.arange(queries, dtype=jnp.int32)[None, :]) & (valid[:, None] == 1)
    ).astype(jnp.bfloat16)
    selector_t = (
        (jnp.arange(queries, dtype=jnp.int32)[:, None] == segment[None, :]) & (valid[None, :] == 1)
    ).astype(jnp.bfloat16)
    partial_value = _module_sums(acts, grads_out, proj_in, proj_out, selector_t)
    summed = _allreduce(partial_value, size, 2)
    precond_cols = jnp.einsum("qmk,mck->qmc", summed, fisher_inv, precision=lax.Precision.HIGH)
    scores = jnp.einsum(
        "qmk,nmk->qn",
        _allgather(precond_cols, size),
        database,
        precision=lax.Precision.HIGH,
    )
    db_count = database.shape[0] * size
    moments = _butterfly_sum(
        jnp.stack([jnp.sum(scores, axis=1), jnp.sum(scores * scores, axis=1)]), size
    )
    avg_score = moments[0] / db_count
    variance = moments[1] / db_count - avg_score * avg_score
    centred = scores - avg_score[:, None]
    return centred * lax.rsqrt(variance + 1e-06)[:, None]


def solution(mesh):
    size = mesh.shape["rows"]
    placed = (
        P(("groups", "rows"), None, None),
        P(("groups", "rows"), None, None),
        P("groups"),
        P(("groups", "rows")),
        P(),
        P(),
        P(None, "rows", None),
        P(("groups", "rows"), None, None),
    )
    return jax.shard_map(
        lambda *a: shards(size, *a),
        mesh=mesh,
        in_specs=placed,
        out_specs=P(None, ("groups", "rows")),
        check_vma=False,
    )
```

```python
import jax
import jax.numpy as jnp
from jax import lax
from jax.experimental import pallas as pl
from jax.experimental.pallas import tpu as pltpu
from jax.sharding import PartitionSpec as P


def _xor_pairs(size, bit):
    return [(i, i ^ (1 << bit)) for i in range(size)]


def _steps(size):
    steps = size.bit_length() - 1
    assert (1 << steps) == size
    return steps


def _join(mine, other, low, axis):
    return jnp.where(
        low, jnp.concatenate([mine, other], axis), jnp.concatenate([other, mine], axis)
    )


def _allreduce(x, size, axis):
    me = lax.axis_index("rows")
    steps = _steps(size)
    cur = x
    for s in range(steps):
        half = cur.shape[axis] // 2
        lo = lax.slice_in_dim(cur, 0, half, axis=axis)
        hi = lax.slice_in_dim(cur, half, 2 * half, axis=axis)
        low = ((me >> s) & 1) == 0
        keep = jnp.where(low, lo, hi)
        send = jnp.where(low, hi, lo)
        cur = keep + lax.ppermute(send, "rows", _xor_pairs(size, s))
    for s in reversed(range(steps)):
        low = ((me >> s) & 1) == 0
        cur = _join(cur, lax.ppermute(cur, "rows", _xor_pairs(size, s)), low, axis)
    return cur


def _allgather(x, size):
    me = lax.axis_index("rows")
    cur = x
    for s in reversed(range(_steps(size))):
        low = ((me >> s) & 1) == 0
        other = lax.ppermute(cur, "rows", _xor_pairs(size, s))
        cur = jnp.where(low, jnp.stack([cur, other], -2), jnp.stack([other, cur], -2))
    return cur.reshape(*x.shape[:-1], size * x.shape[-1])


def _bf16_round(x):
    return lax.reduce_precision(x, exponent_bits=8, mantissa_bits=7)


def _butterfly_sum(x, size):
    for s in range(_steps(size)):
        x = x + lax.ppermute(x, "rows", _xor_pairs(size, s))
    return x


def _sums_kernel(acts_ref, gout_ref, pin_ref, pout_ref, sel_ref, out_ref, act_scr, grad_scr):
    tokens, modules, width_in = acts_ref.shape
    rank = pin_ref.shape[1] // modules
    width = rank * rank
    act_scr[...] = jnp.dot(
        acts_ref[...].reshape(tokens * modules, width_in), pin_ref[...],
        preferred_element_type=jnp.float32,
    )
    grad_scr[...] = jnp.dot(
        gout_ref[...].reshape(tokens * modules, width_in), pout_ref[...],
        preferred_element_type=jnp.float32,
    )
    col = lax.broadcasted_iota(jnp.int32, (modules * rank, width), 1)
    row = lax.broadcasted_iota(jnp.int32, (modules * rank, width), 0)
    sel = sel_ref[...]
    for m in range(modules):
        repeat = (m * rank + col // rank == row).astype(jnp.bfloat16)
        tile = (m * rank + col % rank == row).astype(jnp.bfloat16)
        rows = pl.ds(m, tokens, stride=modules)
        act_proj = act_scr[rows, :].astype(jnp.bfloat16)
        grad_proj = grad_scr[rows, :].astype(jnp.bfloat16)
        act_wide = jnp.dot(act_proj, tile, preferred_element_type=jnp.float32)
        grad_wide = jnp.dot(grad_proj, repeat, preferred_element_type=jnp.float32)
        outer = grad_wide * act_wide
        high = outer.astype(jnp.bfloat16)
        low = (outer - high.astype(jnp.float32)).astype(jnp.bfloat16)
        out_ref[:, m, :] = jnp.dot(sel, high, preferred_element_type=jnp.float32) + jnp.dot(
            sel, low, preferred_element_type=jnp.float32
        )


def _module_sums(acts, grads_out, proj_in, proj_out, selector_t):
    queries = selector_t.shape[0]
    tokens, modules, _ = acts.shape
    rank = proj_in.shape[1] // modules
    scratch = pltpu.VMEM((tokens * modules, modules * rank), jnp.float32)
    return pl.pallas_call(
        _sums_kernel,
        out_shape=jax.ShapeDtypeStruct((queries, modules, rank * rank), jnp.float32),
        scratch_shapes=[scratch, scratch],
    )(acts, grads_out, proj_in, proj_out, selector_t)


def shards(size, acts, grads_out, lengths, valid, proj_in, proj_out, fisher_inv, database):
    tok_rows = acts.shape[0]
    modules = acts.shape[1]
    proj_rank = proj_in.shape[1] // modules
    queries = lengths.shape[0]
    flat_width = proj_rank * proj_rank
    first_pos = lax.axis_index("rows") * tok_rows
    positions = first_pos + jnp.arange(tok_rows, dtype=jnp.int32)
    seg_ends = jnp.cumsum(lengths)
    segment = jnp.sum((seg_ends[None, :] <= positions[:, None]).astype(jnp.int32), axis=1)
    selector = (
        (segment[:, None] == jnp.arange(queries, dtype=jnp.int32)[None, :]) & (valid[:, None] == 1)
    ).astype(jnp.bfloat16)
    selector_t = (
        (jnp.arange(queries, dtype=jnp.int32)[:, None] == segment[None, :]) & (valid[None, :] == 1)
    ).astype(jnp.bfloat16)
    partial_value = _module_sums(acts, grads_out, proj_in, proj_out, selector_t)
    summed = _allreduce(partial_value, size, 2)
    precond_cols = jnp.einsum("qmk,mck->qmc", summed, fisher_inv, precision=lax.Precision.HIGH)
    scores = jnp.einsum(
        "qmk,nmk->qn",
        _allgather(precond_cols, size),
        database,
        precision=lax.Precision.HIGH,
    )
    db_count = database.shape[0] * size
    moments = _butterfly_sum(
        jnp.stack([jnp.sum(scores, axis=1), jnp.sum(scores * scores, axis=1)]), size
    )
    avg_score = moments[0] / db_count
    variance = moments[1] / db_count - avg_score * avg_score
    centred = scores - avg_score[:, None]
    return centred * lax.rsqrt(variance + 1e-06)[:, None]


def solution(mesh):
    size = mesh.shape["rows"]
    placed = (
        P(("groups", "rows"), None, None),
        P(("groups", "rows"), None, None),
        P("groups"),
        P(("groups", "rows")),
        P(),
        P(),
        P(None, "rows", None),
        P(("groups", "rows"), None, None),
    )
    return jax.shard_map(
        lambda *a: shards(size, *a),
        mesh=mesh,
        in_specs=placed,
        out_specs=P(None, ("groups", "rows")),
        check_vma=False,
    )
```

```python
import jax
import jax.numpy as jnp
from jax import lax
from jax.experimental import pallas as pl
from jax.experimental.pallas import tpu as pltpu
from jax.sharding import PartitionSpec as P


def _xor_pairs(size, bit):
    return [(i, i ^ (1 << bit)) for i in range(size)]


def _steps(size):
    steps = size.bit_length() - 1
    assert (1 << steps) == size
    return steps


def _join(mine, other, low, axis):
    return jnp.where(
        low, jnp.concatenate([mine, other], axis), jnp.concatenate([other, mine], axis)
    )


def _allreduce(x, size, axis):
    me = lax.axis_index("rows")
    steps = _steps(size)
    cur = x
    for s in range(steps):
        half = cur.shape[axis] // 2
        lo = lax.slice_in_dim(cur, 0, half, axis=axis)
        hi = lax.slice_in_dim(cur, half, 2 * half, axis=axis)
        low = ((me >> s) & 1) == 0
        keep = jnp.where(low, lo, hi)
        send = jnp.where(low, hi, lo)
        cur = keep + lax.ppermute(send, "rows", _xor_pairs(size, s))
    for s in reversed(range(steps)):
        low = ((me >> s) & 1) == 0
        cur = _join(cur, lax.ppermute(cur, "rows", _xor_pairs(size, s)), low, axis)
    return cur


def _allgather(x, size):
    me = lax.axis_index("rows")
    cur = x
    for s in reversed(range(_steps(size))):
        low = ((me >> s) & 1) == 0
        other = lax.ppermute(cur, "rows", _xor_pairs(size, s))
        cur = jnp.where(low, jnp.stack([cur, other], -2), jnp.stack([other, cur], -2))
    return cur.reshape(*x.shape[:-1], size * x.shape[-1])


def _bf16_round(x):
    return lax.reduce_precision(x, exponent_bits=8, mantissa_bits=7)


def _split(x):
    high = _bf16_round(x)
    return high.astype(jnp.bfloat16), (x - high).astype(jnp.bfloat16)


def _dot3(spec, x, y_high, y_low):
    x_high, x_low = _split(x)
    f = lambda a, b: jnp.einsum(spec, a, b, preferred_element_type=jnp.float32)
    return f(x_high, y_high) + (f(x_low, y_high) + f(x_high, y_low))


def _butterfly_sum(x, size):
    for s in range(_steps(size)):
        x = x + lax.ppermute(x, "rows", _xor_pairs(size, s))
    return x


def _sums_kernel(acts_ref, gout_ref, pin_ref, pout_ref, sel_ref, out_ref, act_scr, grad_scr):
    tokens, modules, width_in = acts_ref.shape
    rank = pin_ref.shape[1] // modules
    width = rank * rank
    act_scr[...] = jnp.dot(
        acts_ref[...].reshape(tokens * modules, width_in), pin_ref[...],
        preferred_element_type=jnp.float32,
    )
    grad_scr[...] = jnp.dot(
        gout_ref[...].reshape(tokens * modules, width_in), pout_ref[...],
        preferred_element_type=jnp.float32,
    )
    col = lax.broadcasted_iota(jnp.int32, (modules * rank, width), 1)
    row = lax.broadcasted_iota(jnp.int32, (modules * rank, width), 0)
    sel = sel_ref[...]
    for m in range(modules):
        repeat = (m * rank + col // rank == row).astype(jnp.bfloat16)
        tile = (m * rank + col % rank == row).astype(jnp.bfloat16)
        rows = pl.ds(m, tokens, stride=modules)
        act_proj = act_scr[rows, :].astype(jnp.bfloat16)
        grad_proj = grad_scr[rows, :].astype(jnp.bfloat16)
        act_wide = jnp.dot(act_proj, tile, preferred_element_type=jnp.float32)
        grad_wide = jnp.dot(grad_proj, repeat, preferred_element_type=jnp.float32)
        outer = grad_wide * act_wide
        high = outer.astype(jnp.bfloat16)
        low = (outer - high.astype(jnp.float32)).astype(jnp.bfloat16)
        out_ref[:, m, :] = jnp.dot(sel, high, preferred_element_type=jnp.float32) + jnp.dot(
            sel, low, preferred_element_type=jnp.float32
        )


def _module_sums(acts, grads_out, proj_in, proj_out, selector_t):
    queries = selector_t.shape[0]
    tokens, modules, _ = acts.shape
    rank = proj_in.shape[1] // modules
    scratch = pltpu.VMEM((tokens * modules, modules * rank), jnp.float32)
    return pl.pallas_call(
        _sums_kernel,
        out_shape=jax.ShapeDtypeStruct((queries, modules, rank * rank), jnp.float32),
        scratch_shapes=[scratch, scratch],
    )(acts, grads_out, proj_in, proj_out, selector_t)


def shards(size, acts, grads_out, lengths, valid, proj_in, proj_out, fisher_inv, database):
    tok_rows = acts.shape[0]
    modules = acts.shape[1]
    proj_rank = proj_in.shape[1] // modules
    queries = lengths.shape[0]
    flat_width = proj_rank * proj_rank
    first_pos = lax.axis_index("rows") * tok_rows
    positions = first_pos + jnp.arange(tok_rows, dtype=jnp.int32)
    seg_ends = jnp.cumsum(lengths)
    segment = jnp.sum((seg_ends[None, :] <= positions[:, None]).astype(jnp.int32), axis=1)
    selector = (
        (segment[:, None] == jnp.arange(queries, dtype=jnp.int32)[None, :]) & (valid[:, None] == 1)
    ).astype(jnp.bfloat16)
    selector_t = (
        (jnp.arange(queries, dtype=jnp.int32)[:, None] == segment[None, :]) & (valid[None, :] == 1)
    ).astype(jnp.bfloat16)
    partial_value = _module_sums(acts, grads_out, proj_in, proj_out, selector_t)
    summed = _allreduce(partial_value, size, 2)
    precond_cols = _dot3("qmk,mck->qmc", summed, *_split(fisher_inv))
    scores = _dot3("qmk,nmk->qn", _allgather(precond_cols, size), *_split(database))
    db_count = database.shape[0] * size
    moments = _butterfly_sum(
        jnp.stack([jnp.sum(scores, axis=1), jnp.sum(scores * scores, axis=1)]), size
    )
    avg_score = moments[0] / db_count
    variance = moments[1] / db_count - avg_score * avg_score
    centred = scores - avg_score[:, None]
    return centred * lax.rsqrt(variance + 1e-06)[:, None]


def solution(mesh):
    size = mesh.shape["rows"]
    placed = (
        P(("groups", "rows"), None, None),
        P(("groups", "rows"), None, None),
        P("groups"),
        P(("groups", "rows")),
        P(),
        P(),
        P(None, "rows", None),
        P(("groups", "rows"), None, None),
    )
    return jax.shard_map(
        lambda *a: shards(size, *a),
        mesh=mesh,
        in_specs=placed,
        out_specs=P(None, ("groups", "rows")),
        check_vma=False,
    )
```

```python
import jax
import jax.numpy as jnp
from jax import lax
from jax.experimental import pallas as pl
from jax.experimental.pallas import tpu as pltpu
from jax.sharding import PartitionSpec as P


def _xor_pairs(size, bit):
    return [(i, i ^ (1 << bit)) for i in range(size)]


def _steps(size):
    steps = size.bit_length() - 1
    assert (1 << steps) == size
    return steps


def _join(mine, other, low, axis):
    return jnp.where(
        low, jnp.concatenate([mine, other], axis), jnp.concatenate([other, mine], axis)
    )


def _orders(size):
    steps = _steps(size)
    first = list(range(steps))
    second = list(first)
    if steps >= 3:
        second[1], second[2] = second[2], second[1]
    return first, second


def _pairs(size, orders, t):
    return [(i, i ^ (1 << orders[i & 1][t])) for i in range(size)]


def _allreduce(x, size, axis):
    me = lax.axis_index("rows")
    orders = _orders(size)
    steps = _steps(size)
    bits = [jnp.where((me & 1) == 0, (me >> orders[0][t]) & 1, (me >> orders[1][t]) & 1) for t in range(steps)]
    cur = x
    for t in range(steps):
        half = cur.shape[axis] // 2
        lo = lax.slice_in_dim(cur, 0, half, axis=axis)
        hi = lax.slice_in_dim(cur, half, 2 * half, axis=axis)
        low = bits[t] == 0
        keep = jnp.where(low, lo, hi)
        send = jnp.where(low, hi, lo)
        cur = keep + lax.ppermute(send, "rows", _pairs(size, orders, t))
    for t in reversed(range(steps)):
        low = bits[t] == 0
        cur = _join(cur, lax.ppermute(cur, "rows", _pairs(size, orders, t)), low, axis)
    return cur


def _allgather(x, size):
    me = lax.axis_index("rows")
    cur = x
    for s in reversed(range(_steps(size))):
        low = ((me >> s) & 1) == 0
        other = lax.ppermute(cur, "rows", _xor_pairs(size, s))
        cur = jnp.where(low, jnp.stack([cur, other], -2), jnp.stack([other, cur], -2))
    return cur.reshape(*x.shape[:-1], size * x.shape[-1])


def _bf16_round(x):
    return lax.reduce_precision(x, exponent_bits=8, mantissa_bits=7)


def _butterfly_sum(x, size):
    for s in range(_steps(size)):
        x = x + lax.ppermute(x, "rows", _xor_pairs(size, s))
    return x


def _sums_kernel(acts_ref, gout_ref, pin_ref, pout_ref, sel_ref, out_ref, act_scr, grad_scr):
    tokens, modules, width_in = acts_ref.shape
    rank = pin_ref.shape[1] // modules
    width = rank * rank
    act_scr[...] = jnp.dot(
        acts_ref[...].reshape(tokens * modules, width_in), pin_ref[...],
        preferred_element_type=jnp.float32,
    )
    grad_scr[...] = jnp.dot(
        gout_ref[...].reshape(tokens * modules, width_in), pout_ref[...],
        preferred_element_type=jnp.float32,
    )
    col = lax.broadcasted_iota(jnp.int32, (modules * rank, width), 1)
    row = lax.broadcasted_iota(jnp.int32, (modules * rank, width), 0)
    sel = sel_ref[...]
    for m in range(modules):
        repeat = (m * rank + col // rank == row).astype(jnp.bfloat16)
        tile = (m * rank + col % rank == row).astype(jnp.bfloat16)
        rows = pl.ds(m, tokens, stride=modules)
        act_proj = act_scr[rows, :].astype(jnp.bfloat16)
        grad_proj = grad_scr[rows, :].astype(jnp.bfloat16)
        act_wide = jnp.dot(act_proj, tile, preferred_element_type=jnp.float32)
        grad_wide = jnp.dot(grad_proj, repeat, preferred_element_type=jnp.float32)
        outer = grad_wide * act_wide
        high = outer.astype(jnp.bfloat16)
        low = (outer - high.astype(jnp.float32)).astype(jnp.bfloat16)
        out_ref[:, m, :] = jnp.dot(sel, high, preferred_element_type=jnp.float32) + jnp.dot(
            sel, low, preferred_element_type=jnp.float32
        )


def _module_sums(acts, grads_out, proj_in, proj_out, selector_t):
    queries = selector_t.shape[0]
    tokens, modules, _ = acts.shape
    rank = proj_in.shape[1] // modules
    scratch = pltpu.VMEM((tokens * modules, modules * rank), jnp.float32)
    return pl.pallas_call(
        _sums_kernel,
        out_shape=jax.ShapeDtypeStruct((queries, modules, rank * rank), jnp.float32),
        scratch_shapes=[scratch, scratch],
    )(acts, grads_out, proj_in, proj_out, selector_t)


def shards(size, acts, grads_out, lengths, valid, proj_in, proj_out, fisher_inv, database):
    tok_rows = acts.shape[0]
    modules = acts.shape[1]
    proj_rank = proj_in.shape[1] // modules
    queries = lengths.shape[0]
    flat_width = proj_rank * proj_rank
    first_pos = lax.axis_index("rows") * tok_rows
    positions = first_pos + jnp.arange(tok_rows, dtype=jnp.int32)
    seg_ends = jnp.cumsum(lengths)
    segment = jnp.sum((seg_ends[None, :] <= positions[:, None]).astype(jnp.int32), axis=1)
    selector = (
        (segment[:, None] == jnp.arange(queries, dtype=jnp.int32)[None, :]) & (valid[:, None] == 1)
    ).astype(jnp.bfloat16)
    selector_t = (
        (jnp.arange(queries, dtype=jnp.int32)[:, None] == segment[None, :]) & (valid[None, :] == 1)
    ).astype(jnp.bfloat16)
    partial_value = _module_sums(acts, grads_out, proj_in, proj_out, selector_t)
    summed = _allreduce(partial_value, size, 2)
    precond_cols = jnp.einsum("qmk,mck->qmc", summed, fisher_inv, precision=lax.Precision.HIGH)
    scores = jnp.einsum(
        "qmk,nmk->qn",
        _allgather(precond_cols, size),
        database,
        precision=lax.Precision.HIGH,
    )
    db_count = database.shape[0] * size
    moments = _butterfly_sum(
        jnp.stack([jnp.sum(scores, axis=1), jnp.sum(scores * scores, axis=1)]), size
    )
    avg_score = moments[0] / db_count
    variance = moments[1] / db_count - avg_score * avg_score
    centred = scores - avg_score[:, None]
    return centred * lax.rsqrt(variance + 1e-06)[:, None]


def solution(mesh):
    size = mesh.shape["rows"]
    placed = (
        P(("groups", "rows"), None, None),
        P(("groups", "rows"), None, None),
        P("groups"),
        P(("groups", "rows")),
        P(),
        P(),
        P(None, "rows", None),
        P(("groups", "rows"), None, None),
    )
    return jax.shard_map(
        lambda *a: shards(size, *a),
        mesh=mesh,
        in_specs=placed,
        out_specs=P(None, ("groups", "rows")),
        check_vma=False,
    )
```

```python
import jax
import jax.numpy as jnp
from jax import lax
from jax.experimental import pallas as pl
from jax.experimental.pallas import tpu as pltpu
from jax.sharding import PartitionSpec as P


def _xor_pairs(size, bit):
    return [(i, i ^ (1 << bit)) for i in range(size)]


def _steps(size):
    steps = size.bit_length() - 1
    assert (1 << steps) == size
    return steps


def _join(mine, other, low, axis):
    return jnp.where(
        low, jnp.concatenate([mine, other], axis), jnp.concatenate([other, mine], axis)
    )


def _orders(size):
    steps = _steps(size)
    first = list(range(steps))
    second = list(first)
    if steps >= 3:
        second[1], second[2] = second[2], second[1]
    return first, second


def _pairs(size, orders, t):
    return [(i, i ^ (1 << orders[i & 1][t])) for i in range(size)]


def _allreduce(keep, send, size, axis):
    me = lax.axis_index("rows")
    orders = _orders(size)
    steps = _steps(size)
    bits = [jnp.where((me & 1) == 0, (me >> orders[0][t]) & 1, (me >> orders[1][t]) & 1) for t in range(steps)]
    cur = keep + lax.ppermute(send, "rows", _pairs(size, orders, 0))
    for t in range(1, steps):
        half = cur.shape[axis] // 2
        lo = lax.slice_in_dim(cur, 0, half, axis=axis)
        hi = lax.slice_in_dim(cur, half, 2 * half, axis=axis)
        low = bits[t] == 0
        keep = jnp.where(low, lo, hi)
        send = jnp.where(low, hi, lo)
        cur = keep + lax.ppermute(send, "rows", _pairs(size, orders, t))
    for t in reversed(range(steps)):
        low = bits[t] == 0
        cur = _join(cur, lax.ppermute(cur, "rows", _pairs(size, orders, t)), low, axis)
    return cur


def _allgather(x, size):
    me = lax.axis_index("rows")
    cur = x
    for s in reversed(range(_steps(size))):
        low = ((me >> s) & 1) == 0
        other = lax.ppermute(cur, "rows", _xor_pairs(size, s))
        cur = jnp.where(low, jnp.stack([cur, other], -2), jnp.stack([other, cur], -2))
    return cur.reshape(*x.shape[:-1], size * x.shape[-1])


def _bf16_round(x):
    return lax.reduce_precision(x, exponent_bits=8, mantissa_bits=7)


def _butterfly_sum(x, size):
    for s in range(_steps(size)):
        x = x + lax.ppermute(x, "rows", _xor_pairs(size, s))
    return x


def _sums_kernel(len_ref, valid_ref, acts_ref, gout_ref, pin_ref, pout_ref, keep_ref, send_ref, act_scr, grad_scr):
    tokens, modules, width_in = acts_ref.shape
    queries = len_ref.shape[1]
    rank = pin_ref.shape[1] // modules
    width = rank * rank
    half = width // 2
    me = lax.axis_index("rows")
    act_scr[...] = jnp.dot(
        acts_ref[...].reshape(tokens * modules, width_in), pin_ref[...],
        preferred_element_type=jnp.float32,
    )
    grad_scr[...] = jnp.dot(
        gout_ref[...].reshape(tokens * modules, width_in), pout_ref[...],
        preferred_element_type=jnp.float32,
    )
    qrow = lax.broadcasted_iota(jnp.int32, (queries, queries), 0)
    qcol = lax.broadcasted_iota(jnp.int32, (queries, queries), 1)
    lengths = jnp.broadcast_to(len_ref[...], (queries, queries))
    ends = jnp.sum(jnp.where(qcol <= qrow, lengths, 0), axis=1, keepdims=True)
    pos = lax.broadcasted_iota(jnp.int32, (queries, tokens), 1) + me * tokens
    segment = jnp.sum((ends <= pos).astype(jnp.int32), axis=0, keepdims=True)
    qid = lax.broadcasted_iota(jnp.int32, (queries, tokens), 0)
    sel = ((segment == qid) & (valid_ref[...] == 1)).astype(jnp.bfloat16)
    col = lax.broadcasted_iota(jnp.int32, (modules * rank, width), 1)
    row = lax.broadcasted_iota(jnp.int32, (modules * rank, width), 0)
    first = (me % 2) == 0
    for m in range(modules):
        repeat = (m * rank + col // rank == row).astype(jnp.bfloat16)
        tile = (m * rank + col % rank == row).astype(jnp.bfloat16)
        rows = pl.ds(m, tokens, stride=modules)
        act_proj = act_scr[rows, :].astype(jnp.bfloat16)
        grad_proj = grad_scr[rows, :].astype(jnp.bfloat16)
        act_wide = jnp.dot(act_proj, tile, preferred_element_type=jnp.float32)
        grad_wide = jnp.dot(grad_proj, repeat, preferred_element_type=jnp.float32)
        outer = grad_wide * act_wide
        high = outer.astype(jnp.bfloat16)
        low = (outer - high.astype(jnp.float32)).astype(jnp.bfloat16)
        total = jnp.dot(sel, high, preferred_element_type=jnp.float32) + jnp.dot(
            sel, low, preferred_element_type=jnp.float32
        )
        lo, hi = total[:, :half], total[:, half:]
        keep_ref[:, m, :] = jnp.where(first, lo, hi)
        send_ref[:, m, :] = jnp.where(first, hi, lo)


def _module_sums(lengths, valid, acts, grads_out, proj_in, proj_out):
    queries = lengths.shape[0]
    tokens, modules, _ = acts.shape
    rank = proj_in.shape[1] // modules
    scratch = pltpu.VMEM((tokens * modules, modules * rank), jnp.float32)
    half = jax.ShapeDtypeStruct((queries, modules, rank * rank // 2), jnp.float32)
    return pl.pallas_call(
        _sums_kernel,
        out_shape=(half, half),
        scratch_shapes=[scratch, scratch],
    )(lengths.reshape(1, queries), valid.reshape(1, tokens), acts, grads_out, proj_in, proj_out)


def shards(size, acts, grads_out, lengths, valid, proj_in, proj_out, fisher_inv, database):
    tok_rows = acts.shape[0]
    modules = acts.shape[1]
    proj_rank = proj_in.shape[1] // modules
    queries = lengths.shape[0]
    flat_width = proj_rank * proj_rank
    keep, send = _module_sums(lengths, valid, acts, grads_out, proj_in, proj_out)
    summed = _allreduce(keep, send, size, 2)
    precond_cols = jnp.einsum("qmk,mck->qmc", summed, fisher_inv, precision=lax.Precision.HIGH)
    scores = jnp.einsum(
        "qmk,nmk->qn",
        _allgather(precond_cols, size),
        database,
        precision=lax.Precision.HIGH,
    )
    db_count = database.shape[0] * size
    moments = _butterfly_sum(
        jnp.stack([jnp.sum(scores, axis=1), jnp.sum(scores * scores, axis=1)]), size
    )
    avg_score = moments[0] / db_count
    variance = moments[1] / db_count - avg_score * avg_score
    centred = scores - avg_score[:, None]
    return centred * lax.rsqrt(variance + 1e-06)[:, None]


def solution(mesh):
    size = mesh.shape["rows"]
    placed = (
        P(("groups", "rows"), None, None),
        P(("groups", "rows"), None, None),
        P("groups"),
        P(("groups", "rows")),
        P(),
        P(),
        P(None, "rows", None),
        P(("groups", "rows"), None, None),
    )
    return jax.shard_map(
        lambda *a: shards(size, *a),
        mesh=mesh,
        in_specs=placed,
        out_specs=P(None, ("groups", "rows")),
        check_vma=False,
    )
```

```python
import jax
import jax.numpy as jnp
from jax import lax
from jax.experimental import pallas as pl
from jax.experimental.pallas import tpu as pltpu
from jax.sharding import PartitionSpec as P


def _xor_pairs(size, bit):
    return [(i, i ^ (1 << bit)) for i in range(size)]


def _steps(size):
    steps = size.bit_length() - 1
    assert (1 << steps) == size
    return steps


def _join(mine, other, low, axis):
    return jnp.where(
        low, jnp.concatenate([mine, other], axis), jnp.concatenate([other, mine], axis)
    )


def _orders(size):
    steps = _steps(size)
    first = list(range(steps))
    second = list(first)
    if steps >= 3:
        second[1], second[2] = second[2], second[1]
    return first, second


def _pairs(size, orders, t):
    return [(i, i ^ (1 << orders[i & 1][t])) for i in range(size)]


def _allreduce_apply(keep, send, size, apply):
    me = lax.axis_index("rows")
    orders = _orders(size)
    steps = _steps(size)
    bits = [jnp.where((me & 1) == 0, (me >> orders[0][t]) & 1, (me >> orders[1][t]) & 1) for t in range(steps)]
    width = 2 * keep.shape[-1]
    base = bits[0] * (width // 2)
    cur = keep + lax.ppermute(send, "rows", _pairs(size, orders, 0))
    for t in range(1, steps):
        half = cur.shape[-1] // 2
        lo = cur[..., :half]
        hi = cur[..., half:]
        low = bits[t] == 0
        keep = jnp.where(low, lo, hi)
        send = jnp.where(low, hi, lo)
        base = base + bits[t] * half
        cur = keep + lax.ppermute(send, "rows", _pairs(size, orders, t))
    total = apply(cur, base)
    for t in reversed(range(steps)):
        low = bits[t] == 0
        span = cur.shape[-1]
        other = lax.ppermute(cur, "rows", _pairs(size, orders, t))
        total = total + apply(other, jnp.where(low, base + span, base - span))
        if t:
            cur = _join(cur, other, low, cur.ndim - 1)
            base = jnp.where(low, base, base - span)
    return total


def _allgather(x, size):
    me = lax.axis_index("rows")
    cur = x
    for s in reversed(range(_steps(size))):
        low = ((me >> s) & 1) == 0
        other = lax.ppermute(cur, "rows", _xor_pairs(size, s))
        cur = jnp.where(low, jnp.stack([cur, other], -2), jnp.stack([other, cur], -2))
    return cur.reshape(*x.shape[:-1], size * x.shape[-1])


def _bf16_round(x):
    return lax.reduce_precision(x, exponent_bits=8, mantissa_bits=7)


def _butterfly_sum(x, size):
    for s in range(_steps(size)):
        x = x + lax.ppermute(x, "rows", _xor_pairs(size, s))
    return x


def _sums_kernel(len_ref, valid_ref, acts_ref, gout_ref, pin_ref, pout_ref, keep_ref, send_ref, act_scr, grad_scr):
    tokens, modules, width_in = acts_ref.shape
    queries = len_ref.shape[1]
    rank = pin_ref.shape[1] // modules
    width = rank * rank
    half = width // 2
    me = lax.axis_index("rows")
    act_scr[...] = jnp.dot(
        acts_ref[...].reshape(tokens * modules, width_in), pin_ref[...],
        preferred_element_type=jnp.float32,
    )
    grad_scr[...] = jnp.dot(
        gout_ref[...].reshape(tokens * modules, width_in), pout_ref[...],
        preferred_element_type=jnp.float32,
    )
    qrow = lax.broadcasted_iota(jnp.int32, (queries, queries), 0)
    qcol = lax.broadcasted_iota(jnp.int32, (queries, queries), 1)
    lengths = jnp.broadcast_to(len_ref[...], (queries, queries))
    ends = jnp.sum(jnp.where(qcol <= qrow, lengths, 0), axis=1, keepdims=True)
    pos = lax.broadcasted_iota(jnp.int32, (queries, tokens), 1) + me * tokens
    segment = jnp.sum((ends <= pos).astype(jnp.int32), axis=0, keepdims=True)
    qid = lax.broadcasted_iota(jnp.int32, (queries, tokens), 0)
    sel = ((segment == qid) & (valid_ref[...] == 1)).astype(jnp.bfloat16)
    col = lax.broadcasted_iota(jnp.int32, (modules * rank, width), 1)
    row = lax.broadcasted_iota(jnp.int32, (modules * rank, width), 0)
    first = (me % 2) == 0
    for m in range(modules):
        repeat = (m * rank + col // rank == row).astype(jnp.bfloat16)
        tile = (m * rank + col % rank == row).astype(jnp.bfloat16)
        rows = pl.ds(m, tokens, stride=modules)
        act_proj = act_scr[rows, :].astype(jnp.bfloat16)
        grad_proj = grad_scr[rows, :].astype(jnp.bfloat16)
        act_wide = jnp.dot(act_proj, tile, preferred_element_type=jnp.float32)
        grad_wide = jnp.dot(grad_proj, repeat, preferred_element_type=jnp.float32)
        outer = grad_wide * act_wide
        high = outer.astype(jnp.bfloat16)
        low = (outer - high.astype(jnp.float32)).astype(jnp.bfloat16)
        total = jnp.dot(sel, high, preferred_element_type=jnp.float32) + jnp.dot(
            sel, low, preferred_element_type=jnp.float32
        )
        lo, hi = total[:, :half], total[:, half:]
        keep_ref[:, m, :] = jnp.where(first, lo, hi)
        send_ref[:, m, :] = jnp.where(first, hi, lo)


def _module_sums(lengths, valid, acts, grads_out, proj_in, proj_out):
    queries = lengths.shape[0]
    tokens, modules, _ = acts.shape
    rank = proj_in.shape[1] // modules
    scratch = pltpu.VMEM((tokens * modules, modules * rank), jnp.float32)
    half = jax.ShapeDtypeStruct((queries, modules, rank * rank // 2), jnp.float32)
    return pl.pallas_call(
        _sums_kernel,
        out_shape=(half, half),
        scratch_shapes=[scratch, scratch],
    )(lengths.reshape(1, queries), valid.reshape(1, tokens), acts, grads_out, proj_in, proj_out)


def shards(size, acts, grads_out, lengths, valid, proj_in, proj_out, fisher_inv, database):
    tok_rows = acts.shape[0]
    modules = acts.shape[1]
    proj_rank = proj_in.shape[1] // modules
    queries = lengths.shape[0]
    flat_width = proj_rank * proj_rank
    keep, send = _module_sums(lengths, valid, acts, grads_out, proj_in, proj_out)

    def precond_part(piece, offset):
        block = lax.dynamic_slice_in_dim(fisher_inv, offset, piece.shape[-1], axis=2)
        return jnp.einsum("qmk,mck->qmc", piece, block, precision=lax.Precision.HIGH)

    precond_cols = _allreduce_apply(keep, send, size, precond_part)
    scores = jnp.einsum(
        "qmk,nmk->qn",
        _allgather(precond_cols, size),
        database,
        precision=lax.Precision.HIGH,
    )
    db_count = database.shape[0] * size
    moments = _butterfly_sum(
        jnp.stack([jnp.sum(scores, axis=1), jnp.sum(scores * scores, axis=1)]), size
    )
    avg_score = moments[0] / db_count
    variance = moments[1] / db_count - avg_score * avg_score
    centred = scores - avg_score[:, None]
    return centred * lax.rsqrt(variance + 1e-06)[:, None]


def solution(mesh):
    size = mesh.shape["rows"]
    placed = (
        P(("groups", "rows"), None, None),
        P(("groups", "rows"), None, None),
        P("groups"),
        P(("groups", "rows")),
        P(),
        P(),
        P(None, "rows", None),
        P(("groups", "rows"), None, None),
    )
    return jax.shard_map(
        lambda *a: shards(size, *a),
        mesh=mesh,
        in_specs=placed,
        out_specs=P(None, ("groups", "rows")),
        check_vma=False,
    )
```

```python
import jax
import jax.numpy as jnp
from jax import lax
from jax.experimental import pallas as pl
from jax.experimental.pallas import tpu as pltpu
from jax.sharding import PartitionSpec as P


def _xor_pairs(size, bit):
    return [(i, i ^ (1 << bit)) for i in range(size)]


def _steps(size):
    steps = size.bit_length() - 1
    assert (1 << steps) == size
    return steps


def _join(mine, other, low, axis):
    return jnp.where(
        low, jnp.concatenate([mine, other], axis), jnp.concatenate([other, mine], axis)
    )


def _orders(size):
    steps = _steps(size)
    first = list(range(steps))
    second = list(first)
    if steps >= 3:
        second[1], second[2] = second[2], second[1]
    return first, second


def _pairs(size, orders, t):
    return [(i, i ^ (1 << orders[i & 1][t])) for i in range(size)]


def _allreduce(keep, send, size, axis):
    me = lax.axis_index("rows")
    orders = _orders(size)
    steps = _steps(size)
    bits = [jnp.where((me & 1) == 0, (me >> orders[0][t]) & 1, (me >> orders[1][t]) & 1) for t in range(steps)]
    cur = keep + lax.ppermute(send, "rows", _pairs(size, orders, 0))
    for t in range(1, steps):
        half = cur.shape[axis] // 2
        lo = lax.slice_in_dim(cur, 0, half, axis=axis)
        hi = lax.slice_in_dim(cur, half, 2 * half, axis=axis)
        low = bits[t] == 0
        keep = jnp.where(low, lo, hi)
        send = jnp.where(low, hi, lo)
        cur = keep + lax.ppermute(send, "rows", _pairs(size, orders, t))
    for t in reversed(range(steps)):
        low = bits[t] == 0
        cur = _join(cur, lax.ppermute(cur, "rows", _pairs(size, orders, t)), low, axis)
    return cur


def _allgather(x, size):
    me = lax.axis_index("rows")
    cur = x
    for s in reversed(range(_steps(size))):
        low = ((me >> s) & 1) == 0
        other = lax.ppermute(cur, "rows", _xor_pairs(size, s))
        cur = jnp.where(low, jnp.stack([cur, other], -2), jnp.stack([other, cur], -2))
    return cur.reshape(*x.shape[:-1], size * x.shape[-1])


def _bf16_round(x):
    return lax.reduce_precision(x, exponent_bits=8, mantissa_bits=7)


def _butterfly_sum(x, size):
    for s in range(_steps(size)):
        x = x + lax.ppermute(x, "rows", _xor_pairs(size, s))
    return x


def _sums_kernel(len_ref, valid_ref, acts_ref, gout_ref, pin_ref, pout_ref, keep_ref, send_ref, act_scr, grad_scr):
    tokens, modules, width_in = acts_ref.shape
    queries = len_ref.shape[1]
    rank = pin_ref.shape[1] // modules
    width = rank * rank
    half = width // 2
    me = lax.axis_index("rows")
    act_scr[...] = jnp.dot(
        acts_ref[...].reshape(tokens * modules, width_in), pin_ref[...],
        preferred_element_type=jnp.float32,
    )
    grad_scr[...] = jnp.dot(
        gout_ref[...].reshape(tokens * modules, width_in), pout_ref[...],
        preferred_element_type=jnp.float32,
    )
    qrow = lax.broadcasted_iota(jnp.int32, (queries, queries), 0)
    qcol = lax.broadcasted_iota(jnp.int32, (queries, queries), 1)
    lengths = jnp.broadcast_to(len_ref[...], (queries, queries))
    ends = jnp.sum(jnp.where(qcol <= qrow, lengths, 0), axis=1, keepdims=True)
    pos = lax.broadcasted_iota(jnp.int32, (queries, tokens), 1) + me * tokens
    segment = jnp.sum((ends <= pos).astype(jnp.int32), axis=0, keepdims=True)
    qid = lax.broadcasted_iota(jnp.int32, (queries, tokens), 0)
    sel = ((segment == qid) & (valid_ref[...] == 1)).astype(jnp.bfloat16)
    col = lax.broadcasted_iota(jnp.int32, (modules * rank, width), 1)
    row = lax.broadcasted_iota(jnp.int32, (modules * rank, width), 0)
    first = (me % 2) == 0
    for m in range(modules):
        repeat = (m * rank + col // rank == row).astype(jnp.bfloat16)
        tile = (m * rank + col % rank == row).astype(jnp.bfloat16)
        rows = pl.ds(m, tokens, stride=modules)
        act_proj = act_scr[rows, :].astype(jnp.bfloat16)
        grad_proj = grad_scr[rows, :].astype(jnp.bfloat16)
        act_wide = jnp.dot(act_proj, tile, preferred_element_type=jnp.float32)
        grad_wide = jnp.dot(grad_proj, repeat, preferred_element_type=jnp.float32)
        outer = grad_wide * act_wide
        high = outer.astype(jnp.bfloat16)
        low = (outer - high.astype(jnp.float32)).astype(jnp.bfloat16)
        total = jnp.dot(sel, high, preferred_element_type=jnp.float32) + jnp.dot(
            sel, low, preferred_element_type=jnp.float32
        )
        lo, hi = total[:, :half], total[:, half:]
        keep_ref[:, m, :] = jnp.where(first, lo, hi)
        send_ref[:, m, :] = jnp.where(first, hi, lo)


def _module_sums(lengths, valid, acts, grads_out, proj_in, proj_out):
    queries = lengths.shape[0]
    tokens, modules, _ = acts.shape
    rank = proj_in.shape[1] // modules
    scratch = pltpu.VMEM((tokens * modules, modules * rank), jnp.float32)
    half = jax.ShapeDtypeStruct((queries, modules, rank * rank // 2), jnp.float32)
    return pl.pallas_call(
        _sums_kernel,
        out_shape=(half, half),
        scratch_shapes=[scratch, scratch],
    )(lengths.reshape(1, queries), valid.reshape(1, tokens), acts, grads_out, proj_in, proj_out)


def _split_bf16(x):
    high = x.astype(jnp.bfloat16)
    return high, (x - high.astype(jnp.float32)).astype(jnp.bfloat16)


def _scores_kernel(p_ref, db_ref, out_ref):
    modules, width = p_ref.shape[1], p_ref.shape[2]
    chunk = 512
    nt = (((1,), (1,)), ((), ()))
    f = lambda a, b: lax.dot_general(a, b, nt, preferred_element_type=jnp.float32)
    out_ref[...] = jnp.zeros(out_ref.shape, jnp.float32)
    for m in range(modules):
        for c in range(width // chunk):
            cols = pl.ds(c * chunk, chunk)
            p_high, p_low = _split_bf16(p_ref[:, m, cols])
            d_high, d_low = _split_bf16(db_ref[:, m, cols])
            out_ref[...] += f(p_high, d_high) + (f(p_low, d_high) + f(p_high, d_low))


def _scores(precond, database):
    return pl.pallas_call(
        _scores_kernel,
        out_shape=jax.ShapeDtypeStruct((precond.shape[0], database.shape[0]), jnp.float32),
        compiler_params=pltpu.CompilerParams(vmem_limit_bytes=56 * 1024 * 1024),
    )(precond, database)


def shards(size, acts, grads_out, lengths, valid, proj_in, proj_out, fisher_inv, database):
    tok_rows = acts.shape[0]
    modules = acts.shape[1]
    proj_rank = proj_in.shape[1] // modules
    queries = lengths.shape[0]
    flat_width = proj_rank * proj_rank
    keep, send = _module_sums(lengths, valid, acts, grads_out, proj_in, proj_out)
    summed = _allreduce(keep, send, size, 2)
    precond_cols = jnp.einsum("qmk,mck->qmc", summed, fisher_inv, precision=lax.Precision.HIGH)
    scores = _scores(_allgather(precond_cols, size), database)
    db_count = database.shape[0] * size
    moments = _butterfly_sum(
        jnp.stack([jnp.sum(scores, axis=1), jnp.sum(scores * scores, axis=1)]), size
    )
    avg_score = moments[0] / db_count
    variance = moments[1] / db_count - avg_score * avg_score
    centred = scores - avg_score[:, None]
    return centred * lax.rsqrt(variance + 1e-06)[:, None]


def solution(mesh):
    size = mesh.shape["rows"]
    placed = (
        P(("groups", "rows"), None, None),
        P(("groups", "rows"), None, None),
        P("groups"),
        P(("groups", "rows")),
        P(),
        P(),
        P(None, "rows", None),
        P(("groups", "rows"), None, None),
    )
    return jax.shard_map(
        lambda *a: shards(size, *a),
        mesh=mesh,
        in_specs=placed,
        out_specs=P(None, ("groups", "rows")),
        check_vma=False,
    )
```

```python
import jax
import jax.numpy as jnp
from jax import lax
from jax.experimental import pallas as pl
from jax.experimental.pallas import tpu as pltpu
from jax.sharding import PartitionSpec as P


def _xor_pairs(size, bit):
    return [(i, i ^ (1 << bit)) for i in range(size)]


def _steps(size):
    steps = size.bit_length() - 1
    assert (1 << steps) == size
    return steps


def _join(mine, other, low, axis):
    return jnp.where(
        low, jnp.concatenate([mine, other], axis), jnp.concatenate([other, mine], axis)
    )


def _orders(size):
    steps = _steps(size)
    first = list(range(steps))
    second = list(first)
    if steps >= 3:
        second[1], second[2] = second[2], second[1]
    return first, second


def _pairs(size, orders, t):
    return [(i, i ^ (1 << orders[i & 1][t])) for i in range(size)]


def _allreduce(keep, send, size, axis):
    me = lax.axis_index("rows")
    orders = _orders(size)
    steps = _steps(size)
    bits = [jnp.where((me & 1) == 0, (me >> orders[0][t]) & 1, (me >> orders[1][t]) & 1) for t in range(steps)]
    cur = keep + lax.ppermute(send, "rows", _pairs(size, orders, 0))
    for t in range(1, steps):
        half = cur.shape[axis] // 2
        lo = lax.slice_in_dim(cur, 0, half, axis=axis)
        hi = lax.slice_in_dim(cur, half, 2 * half, axis=axis)
        low = bits[t] == 0
        keep = jnp.where(low, lo, hi)
        send = jnp.where(low, hi, lo)
        cur = keep + lax.ppermute(send, "rows", _pairs(size, orders, t))
    for t in reversed(range(steps)):
        low = bits[t] == 0
        cur = _join(cur, lax.ppermute(cur, "rows", _pairs(size, orders, t)), low, axis)
    return cur


def _allgather(x, size):
    me = lax.axis_index("rows")
    cur = x
    for s in reversed(range(_steps(size))):
        low = ((me >> s) & 1) == 0
        other = lax.ppermute(cur, "rows", _xor_pairs(size, s))
        cur = jnp.where(low, jnp.stack([cur, other], -2), jnp.stack([other, cur], -2))
    return cur.reshape(*x.shape[:-1], size * x.shape[-1])


def _bf16_round(x):
    return lax.reduce_precision(x, exponent_bits=8, mantissa_bits=7)


def _butterfly_sum(x, size):
    for s in range(_steps(size)):
        x = x + lax.ppermute(x, "rows", _xor_pairs(size, s))
    return x


def _sums_kernel(len_ref, valid_ref, acts_ref, gout_ref, pin_ref, pout_ref, keep_ref, send_ref, act_scr, grad_scr):
    tokens, modules, width_in = acts_ref.shape
    queries = len_ref.shape[1]
    rank = pin_ref.shape[1] // modules
    width = rank * rank
    half = width // 2
    me = lax.axis_index("rows")
    act_scr[...] = jnp.dot(
        acts_ref[...].reshape(tokens * modules, width_in), pin_ref[...],
        preferred_element_type=jnp.float32,
    )
    grad_scr[...] = jnp.dot(
        gout_ref[...].reshape(tokens * modules, width_in), pout_ref[...],
        preferred_element_type=jnp.float32,
    )
    qrow = lax.broadcasted_iota(jnp.int32, (queries, queries), 0)
    qcol = lax.broadcasted_iota(jnp.int32, (queries, queries), 1)
    lengths = jnp.broadcast_to(len_ref[...], (queries, queries))
    ends = jnp.sum(jnp.where(qcol <= qrow, lengths, 0), axis=1, keepdims=True)
    pos = lax.broadcasted_iota(jnp.int32, (queries, tokens), 1) + me * tokens
    segment = jnp.sum((ends <= pos).astype(jnp.int32), axis=0, keepdims=True)
    qid = lax.broadcasted_iota(jnp.int32, (queries, tokens), 0)
    sel = ((segment == qid) & (valid_ref[...] == 1)).astype(jnp.bfloat16)
    col = lax.broadcasted_iota(jnp.int32, (modules * rank, width), 1)
    row = lax.broadcasted_iota(jnp.int32, (modules * rank, width), 0)
    first = (me % 2) == 0
    for m in range(modules):
        repeat = (m * rank + col // rank == row).astype(jnp.bfloat16)
        tile = (m * rank + col % rank == row).astype(jnp.bfloat16)
        rows = pl.ds(m, tokens, stride=modules)
        act_proj = act_scr[rows, :].astype(jnp.bfloat16)
        grad_proj = grad_scr[rows, :].astype(jnp.bfloat16)
        act_wide = jnp.dot(act_proj, tile, preferred_element_type=jnp.float32)
        grad_wide = jnp.dot(grad_proj, repeat, preferred_element_type=jnp.float32)
        outer = grad_wide * act_wide
        high = outer.astype(jnp.bfloat16)
        low = (outer - high.astype(jnp.float32)).astype(jnp.bfloat16)
        total = jnp.dot(sel, high, preferred_element_type=jnp.float32) + jnp.dot(
            sel, low, preferred_element_type=jnp.float32
        )
        lo, hi = total[:, :half], total[:, half:]
        keep_ref[m] = jnp.where(first, lo, hi)
        send_ref[m] = jnp.where(first, hi, lo)


def _module_sums(lengths, valid, acts, grads_out, proj_in, proj_out):
    queries = lengths.shape[0]
    tokens, modules, _ = acts.shape
    rank = proj_in.shape[1] // modules
    scratch = pltpu.VMEM((tokens * modules, modules * rank), jnp.float32)
    half = jax.ShapeDtypeStruct((modules, queries, rank * rank // 2), jnp.float32)
    return pl.pallas_call(
        _sums_kernel,
        out_shape=(half, half),
        scratch_shapes=[scratch, scratch],
    )(lengths.reshape(1, queries), valid.reshape(1, tokens), acts, grads_out, proj_in, proj_out)


def _split_bf16(x):
    high = x.astype(jnp.bfloat16)
    return high, (x - high.astype(jnp.float32)).astype(jnp.bfloat16)


def _precond_kernel(g_ref, f_ref, out_ref):
    nt = (((1,), (1,)), ((), ()))
    f = lambda a, b: lax.dot_general(a, b, nt, preferred_element_type=jnp.float32)
    for m in range(g_ref.shape[0]):
        g_high, g_low = _split_bf16(g_ref[m])
        f_high, f_low = _split_bf16(f_ref[m])
        out_ref[m] = f(g_high, f_high) + (f(g_low, f_high) + f(g_high, f_low))


def _precond(grads, fisher_inv):
    modules, queries, _ = grads.shape
    return pl.pallas_call(
        _precond_kernel,
        out_shape=jax.ShapeDtypeStruct((modules, queries, fisher_inv.shape[1]), jnp.float32),
        compiler_params=pltpu.CompilerParams(vmem_limit_bytes=48 * 1024 * 1024),
    )(grads, fisher_inv)


def shards(size, acts, grads_out, lengths, valid, proj_in, proj_out, fisher_inv, database):
    tok_rows = acts.shape[0]
    modules = acts.shape[1]
    proj_rank = proj_in.shape[1] // modules
    queries = lengths.shape[0]
    flat_width = proj_rank * proj_rank
    keep, send = _module_sums(lengths, valid, acts, grads_out, proj_in, proj_out)
    summed = _allreduce(keep, send, size, 2)
    precond_cols = _precond(summed, fisher_inv)
    scores = jnp.einsum(
        "mqk,nmk->qn",
        _allgather(precond_cols, size),
        database,
        precision=lax.Precision.HIGH,
    )
    db_count = database.shape[0] * size
    moments = _butterfly_sum(
        jnp.stack([jnp.sum(scores, axis=1), jnp.sum(scores * scores, axis=1)]), size
    )
    avg_score = moments[0] / db_count
    variance = moments[1] / db_count - avg_score * avg_score
    centred = scores - avg_score[:, None]
    return centred * lax.rsqrt(variance + 1e-06)[:, None]


def solution(mesh):
    size = mesh.shape["rows"]
    placed = (
        P(("groups", "rows"), None, None),
        P(("groups", "rows"), None, None),
        P("groups"),
        P(("groups", "rows")),
        P(),
        P(),
        P(None, "rows", None),
        P(("groups", "rows"), None, None),
    )
    return jax.shard_map(
        lambda *a: shards(size, *a),
        mesh=mesh,
        in_specs=placed,
        out_specs=P(None, ("groups", "rows")),
        check_vma=False,
    )
```

```python
import jax
import jax.numpy as jnp
from jax import lax
from jax.experimental import pallas as pl
from jax.experimental.pallas import tpu as pltpu
from jax.sharding import PartitionSpec as P


def _xor_pairs(size, bit):
    return [(i, i ^ (1 << bit)) for i in range(size)]


def _steps(size):
    steps = size.bit_length() - 1
    assert (1 << steps) == size
    return steps


def _join(mine, other, low, axis):
    return jnp.where(
        low, jnp.concatenate([mine, other], axis), jnp.concatenate([other, mine], axis)
    )


def _orders(size):
    steps = _steps(size)
    first = list(range(steps))
    second = list(first)
    if steps >= 3:
        second[1], second[2] = second[2], second[1]
    return first, second


def _pairs(size, orders, t):
    return [(i, i ^ (1 << orders[i & 1][t])) for i in range(size)]


def _allreduce(keep, send, size, axis):
    me = lax.axis_index("rows")
    orders = _orders(size)
    steps = _steps(size)
    bits = [jnp.where((me & 1) == 0, (me >> orders[0][t]) & 1, (me >> orders[1][t]) & 1) for t in range(steps)]
    cur = keep + lax.ppermute(send, "rows", _pairs(size, orders, 0))
    for t in range(1, steps):
        half = cur.shape[axis] // 2
        lo = lax.slice_in_dim(cur, 0, half, axis=axis)
        hi = lax.slice_in_dim(cur, half, 2 * half, axis=axis)
        low = bits[t] == 0
        keep = jnp.where(low, lo, hi)
        send = jnp.where(low, hi, lo)
        cur = keep + lax.ppermute(send, "rows", _pairs(size, orders, t))
    for t in reversed(range(steps)):
        low = bits[t] == 0
        cur = _join(cur, lax.ppermute(cur, "rows", _pairs(size, orders, t)), low, axis)
    return cur


def _allgather(x, size):
    me = lax.axis_index("rows")
    cur = x
    for s in reversed(range(_steps(size))):
        low = ((me >> s) & 1) == 0
        other = lax.ppermute(cur, "rows", _xor_pairs(size, s))
        cur = jnp.where(low, jnp.stack([cur, other], -2), jnp.stack([other, cur], -2))
    return cur.reshape(*x.shape[:-1], size * x.shape[-1])


def _bf16_round(x):
    return lax.reduce_precision(x, exponent_bits=8, mantissa_bits=7)


def _butterfly_sum(x, size):
    for s in range(_steps(size)):
        x = x + lax.ppermute(x, "rows", _xor_pairs(size, s))
    return x


def _sums_kernel(len_ref, valid_ref, acts_ref, gout_ref, pin_ref, pout_ref, keep_ref, send_ref, act_scr, grad_scr):
    tokens, modules, width_in = acts_ref.shape
    queries = len_ref.shape[1]
    rank = pin_ref.shape[1] // modules
    width = rank * rank
    half = width // 2
    me = lax.axis_index("rows")
    act_scr[...] = jnp.dot(
        acts_ref[...].reshape(tokens * modules, width_in), pin_ref[...],
        preferred_element_type=jnp.float32,
    )
    grad_scr[...] = jnp.dot(
        gout_ref[...].reshape(tokens * modules, width_in), pout_ref[...],
        preferred_element_type=jnp.float32,
    )
    qrow = lax.broadcasted_iota(jnp.int32, (queries, queries), 0)
    qcol = lax.broadcasted_iota(jnp.int32, (queries, queries), 1)
    lengths = jnp.broadcast_to(len_ref[...], (queries, queries))
    ends = jnp.sum(jnp.where(qcol <= qrow, lengths, 0), axis=1, keepdims=True)
    pos = lax.broadcasted_iota(jnp.int32, (queries, tokens), 1) + me * tokens
    segment = jnp.sum((ends <= pos).astype(jnp.int32), axis=0, keepdims=True)
    qid = lax.broadcasted_iota(jnp.int32, (queries, tokens), 0)
    sel = ((segment == qid) & (valid_ref[...] == 1)).astype(jnp.bfloat16)
    col = lax.broadcasted_iota(jnp.int32, (modules * rank, width), 1)
    row = lax.broadcasted_iota(jnp.int32, (modules * rank, width), 0)
    first = (me % 2) == 0
    for m in range(modules):
        repeat = (m * rank + col // rank == row).astype(jnp.bfloat16)
        tile = (m * rank + col % rank == row).astype(jnp.bfloat16)
        rows = pl.ds(m, tokens, stride=modules)
        act_proj = act_scr[rows, :].astype(jnp.bfloat16)
        grad_proj = grad_scr[rows, :].astype(jnp.bfloat16)
        act_wide = jnp.dot(act_proj, tile, preferred_element_type=jnp.float32)
        grad_wide = jnp.dot(grad_proj, repeat, preferred_element_type=jnp.float32)
        outer = grad_wide * act_wide
        high = outer.astype(jnp.bfloat16)
        low = (outer - high.astype(jnp.float32)).astype(jnp.bfloat16)
        total = jnp.dot(sel, high, preferred_element_type=jnp.float32) + jnp.dot(
            sel, low, preferred_element_type=jnp.float32
        )
        lo, hi = total[:, :half], total[:, half:]
        keep_ref[m] = jnp.where(first, lo, hi)
        send_ref[m] = jnp.where(first, hi, lo)


def _module_sums(lengths, valid, acts, grads_out, proj_in, proj_out):
    queries = lengths.shape[0]
    tokens, modules, _ = acts.shape
    rank = proj_in.shape[1] // modules
    scratch = pltpu.VMEM((tokens * modules, modules * rank), jnp.float32)
    half = jax.ShapeDtypeStruct((modules, queries, rank * rank // 2), jnp.float32)
    return pl.pallas_call(
        _sums_kernel,
        out_shape=(half, half),
        scratch_shapes=[scratch, scratch],
    )(lengths.reshape(1, queries), valid.reshape(1, tokens), acts, grads_out, proj_in, proj_out)


def _split_bf16(x):
    high = x.astype(jnp.bfloat16)
    return high, (x - high.astype(jnp.float32)).astype(jnp.bfloat16)


def _precond_kernel(g_ref, f_ref, out_ref):
    @pl.when(pl.program_id(0) == 0)
    def _():
        out_ref[...] = jnp.zeros(out_ref.shape, jnp.float32)

    nt = (((1,), (1,)), ((), ()))
    f = lambda a, b: lax.dot_general(a, b, nt, preferred_element_type=jnp.float32)
    for m in range(g_ref.shape[0]):
        g_high, g_low = _split_bf16(g_ref[m])
        f_high, f_low = _split_bf16(f_ref[m])
        out_ref[m] += f(g_high, f_high) + (f(g_low, f_high) + f(g_high, f_low))


def _precond(grads, fisher_inv):
    modules, queries, width = grads.shape
    cols = fisher_inv.shape[1]
    block = min(width, 1024)
    return pl.pallas_call(
        _precond_kernel,
        out_shape=jax.ShapeDtypeStruct((modules, queries, cols), jnp.float32),
        grid=(width // block,),
        in_specs=[
            pl.BlockSpec((modules, queries, block), lambda k: (0, 0, k)),
            pl.BlockSpec((modules, cols, block), lambda k: (0, 0, k)),
        ],
        out_specs=pl.BlockSpec((modules, queries, cols), lambda k: (0, 0, 0)),
    )(grads, fisher_inv)


def shards(size, acts, grads_out, lengths, valid, proj_in, proj_out, fisher_inv, database):
    tok_rows = acts.shape[0]
    modules = acts.shape[1]
    proj_rank = proj_in.shape[1] // modules
    queries = lengths.shape[0]
    flat_width = proj_rank * proj_rank
    keep, send = _module_sums(lengths, valid, acts, grads_out, proj_in, proj_out)
    summed = _allreduce(keep, send, size, 2)
    precond_cols = _precond(summed, fisher_inv)
    scores = jnp.einsum(
        "mqk,nmk->qn",
        _allgather(precond_cols, size),
        database,
        precision=lax.Precision.HIGH,
    )
    db_count = database.shape[0] * size
    moments = _butterfly_sum(
        jnp.stack([jnp.sum(scores, axis=1), jnp.sum(scores * scores, axis=1)]), size
    )
    avg_score = moments[0] / db_count
    variance = moments[1] / db_count - avg_score * avg_score
    centred = scores - avg_score[:, None]
    return centred * lax.rsqrt(variance + 1e-06)[:, None]


def solution(mesh):
    size = mesh.shape["rows"]
    placed = (
        P(("groups", "rows"), None, None),
        P(("groups", "rows"), None, None),
        P("groups"),
        P(("groups", "rows")),
        P(),
        P(),
        P(None, "rows", None),
        P(("groups", "rows"), None, None),
    )
    return jax.shard_map(
        lambda *a: shards(size, *a),
        mesh=mesh,
        in_specs=placed,
        out_specs=P(None, ("groups", "rows")),
        check_vma=False,
    )
```

```python
import jax
import jax.numpy as jnp
from jax import lax
from jax.experimental import pallas as pl
from jax.experimental.pallas import tpu as pltpu
from jax.sharding import PartitionSpec as P


def _xor_pairs(size, bit):
    return [(i, i ^ (1 << bit)) for i in range(size)]


def _steps(size):
    steps = size.bit_length() - 1
    assert (1 << steps) == size
    return steps


def _join(mine, other, low, axis):
    return jnp.where(
        low, jnp.concatenate([mine, other], axis), jnp.concatenate([other, mine], axis)
    )


def _orders(size):
    steps = _steps(size)
    first = list(range(steps))
    second = list(first)
    if steps >= 3:
        second[1], second[2] = second[2], second[1]
    return first, second


def _pairs(size, orders, t):
    return [(i, i ^ (1 << orders[i & 1][t])) for i in range(size)]


def _allreduce(keep, send, size, axis):
    me = lax.axis_index("rows")
    orders = _orders(size)
    steps = _steps(size)
    bits = [jnp.where((me & 1) == 0, (me >> orders[0][t]) & 1, (me >> orders[1][t]) & 1) for t in range(steps)]
    cur = keep + lax.ppermute(send, "rows", _pairs(size, orders, 0))
    for t in range(1, steps):
        half = cur.shape[axis] // 2
        lo = lax.slice_in_dim(cur, 0, half, axis=axis)
        hi = lax.slice_in_dim(cur, half, 2 * half, axis=axis)
        low = bits[t] == 0
        keep = jnp.where(low, lo, hi)
        send = jnp.where(low, hi, lo)
        cur = keep + lax.ppermute(send, "rows", _pairs(size, orders, t))
    for t in reversed(range(steps)):
        low = bits[t] == 0
        cur = _join(cur, lax.ppermute(cur, "rows", _pairs(size, orders, t)), low, axis)
    return cur


def _allgather(x, size):
    me = lax.axis_index("rows")
    steps = _steps(size)
    orders = [list(reversed(o)) for o in _orders(size)]
    lead = x.ndim - 1
    cur = x
    for t in range(steps):
        if t == steps - 1 and orders[0] != orders[1]:
            perm = list(range(cur.ndim))
            a, b = lead + steps - 3, lead + steps - 2
            perm[a], perm[b] = perm[b], perm[a]
            cur = jnp.where((me & 1) == 0, cur, jnp.transpose(cur, perm))
        bit = jnp.where((me & 1) == 0, (me >> orders[0][t]) & 1, (me >> orders[1][t]) & 1)
        other = lax.ppermute(cur, "rows", [(i, i ^ (1 << orders[i & 1][t])) for i in range(size)])
        cur = jnp.where(bit == 0, jnp.stack([cur, other], -2), jnp.stack([other, cur], -2))
    return cur.reshape(*x.shape[:-1], size * x.shape[-1])


def _bf16_round(x):
    return lax.reduce_precision(x, exponent_bits=8, mantissa_bits=7)


def _butterfly_sum(x, size):
    for s in range(_steps(size)):
        x = x + lax.ppermute(x, "rows", _xor_pairs(size, s))
    return x


def _sums_kernel(len_ref, valid_ref, acts_ref, gout_ref, pin_ref, pout_ref, keep_ref, send_ref, act_scr, grad_scr):
    tokens, modules, width_in = acts_ref.shape
    queries = len_ref.shape[1]
    rank = pin_ref.shape[1] // modules
    width = rank * rank
    half = width // 2
    me = lax.axis_index("rows")
    act_scr[...] = jnp.dot(
        acts_ref[...].reshape(tokens * modules, width_in), pin_ref[...],
        preferred_element_type=jnp.float32,
    )
    grad_scr[...] = jnp.dot(
        gout_ref[...].reshape(tokens * modules, width_in), pout_ref[...],
        preferred_element_type=jnp.float32,
    )
    qrow = lax.broadcasted_iota(jnp.int32, (queries, queries), 0)
    qcol = lax.broadcasted_iota(jnp.int32, (queries, queries), 1)
    lengths = jnp.broadcast_to(len_ref[...], (queries, queries))
    ends = jnp.sum(jnp.where(qcol <= qrow, lengths, 0), axis=1, keepdims=True)
    pos = lax.broadcasted_iota(jnp.int32, (queries, tokens), 1) + me * tokens
    segment = jnp.sum((ends <= pos).astype(jnp.int32), axis=0, keepdims=True)
    qid = lax.broadcasted_iota(jnp.int32, (queries, tokens), 0)
    sel = ((segment == qid) & (valid_ref[...] == 1)).astype(jnp.bfloat16)
    col = lax.broadcasted_iota(jnp.int32, (modules * rank, width), 1)
    row = lax.broadcasted_iota(jnp.int32, (modules * rank, width), 0)
    first = (me % 2) == 0
    for m in range(modules):
        repeat = (m * rank + col // rank == row).astype(jnp.bfloat16)
        tile = (m * rank + col % rank == row).astype(jnp.bfloat16)
        rows = pl.ds(m, tokens, stride=modules)
        act_proj = act_scr[rows, :].astype(jnp.bfloat16)
        grad_proj = grad_scr[rows, :].astype(jnp.bfloat16)
        act_wide = jnp.dot(act_proj, tile, preferred_element_type=jnp.float32)
        grad_wide = jnp.dot(grad_proj, repeat, preferred_element_type=jnp.float32)
        outer = grad_wide * act_wide
        high = outer.astype(jnp.bfloat16)
        low = (outer - high.astype(jnp.float32)).astype(jnp.bfloat16)
        total = jnp.dot(sel, high, preferred_element_type=jnp.float32) + jnp.dot(
            sel, low, preferred_element_type=jnp.float32
        )
        lo, hi = total[:, :half], total[:, half:]
        keep_ref[m] = jnp.where(first, lo, hi)
        send_ref[m] = jnp.where(first, hi, lo)


def _module_sums(lengths, valid, acts, grads_out, proj_in, proj_out):
    queries = lengths.shape[0]
    tokens, modules, _ = acts.shape
    rank = proj_in.shape[1] // modules
    scratch = pltpu.VMEM((tokens * modules, modules * rank), jnp.float32)
    half = jax.ShapeDtypeStruct((modules, queries, rank * rank // 2), jnp.float32)
    return pl.pallas_call(
        _sums_kernel,
        out_shape=(half, half),
        scratch_shapes=[scratch, scratch],
    )(lengths.reshape(1, queries), valid.reshape(1, tokens), acts, grads_out, proj_in, proj_out)


def _split_bf16(x):
    high = x.astype(jnp.bfloat16)
    return high, (x - high.astype(jnp.float32)).astype(jnp.bfloat16)


def _precond_kernel(g_ref, f_ref, out_ref):
    nt = (((1,), (1,)), ((), ()))
    f = lambda a, b: lax.dot_general(a, b, nt, preferred_element_type=jnp.float32)
    for m in range(g_ref.shape[0]):
        g_high, g_low = _split_bf16(g_ref[m])
        f_high, f_low = _split_bf16(f_ref[m])
        out_ref[m] = f(g_high, f_high) + (f(g_low, f_high) + f(g_high, f_low))


def _precond(grads, fisher_inv):
    modules, queries, _ = grads.shape
    return pl.pallas_call(
        _precond_kernel,
        out_shape=jax.ShapeDtypeStruct((modules, queries, fisher_inv.shape[1]), jnp.float32),
        compiler_params=pltpu.CompilerParams(vmem_limit_bytes=48 * 1024 * 1024),
    )(grads, fisher_inv)


def shards(size, acts, grads_out, lengths, valid, proj_in, proj_out, fisher_inv, database):
    tok_rows = acts.shape[0]
    modules = acts.shape[1]
    proj_rank = proj_in.shape[1] // modules
    queries = lengths.shape[0]
    flat_width = proj_rank * proj_rank
    keep, send = _module_sums(lengths, valid, acts, grads_out, proj_in, proj_out)
    summed = _allreduce(keep, send, size, 2)
    precond_cols = _precond(summed, fisher_inv)
    scores = jnp.einsum(
        "mqk,nmk->qn",
        _allgather(precond_cols, size),
        database,
        precision=lax.Precision.HIGH,
    )
    db_count = database.shape[0] * size
    moments = _butterfly_sum(
        jnp.stack([jnp.sum(scores, axis=1), jnp.sum(scores * scores, axis=1)]), size
    )
    avg_score = moments[0] / db_count
    variance = moments[1] / db_count - avg_score * avg_score
    centred = scores - avg_score[:, None]
    return centred * lax.rsqrt(variance + 1e-06)[:, None]


def solution(mesh):
    size = mesh.shape["rows"]
    placed = (
        P(("groups", "rows"), None, None),
        P(("groups", "rows"), None, None),
        P("groups"),
        P(("groups", "rows")),
        P(),
        P(),
        P(None, "rows", None),
        P(("groups", "rows"), None, None),
    )
    return jax.shard_map(
        lambda *a: shards(size, *a),
        mesh=mesh,
        in_specs=placed,
        out_specs=P(None, ("groups", "rows")),
        check_vma=False,
    )
```

```python
import jax
import jax.numpy as jnp
from jax import lax
from jax.experimental import pallas as pl
from jax.experimental.pallas import tpu as pltpu
from jax.sharding import PartitionSpec as P


def _xor_pairs(size, bit):
    return [(i, i ^ (1 << bit)) for i in range(size)]


def _steps(size):
    steps = size.bit_length() - 1
    assert (1 << steps) == size
    return steps


def _join(mine, other, low, axis):
    return jnp.where(
        low, jnp.concatenate([mine, other], axis), jnp.concatenate([other, mine], axis)
    )


def _orders(size):
    steps = _steps(size)
    first = list(range(steps))
    second = list(first)
    if steps >= 3:
        second[1], second[2] = second[2], second[1]
    return first, second


def _pairs(size, orders, t):
    return [(i, i ^ (1 << orders[i & 1][t])) for i in range(size)]


def _allreduce(keep, send, size, axis):
    me = lax.axis_index("rows")
    orders = _orders(size)
    steps = _steps(size)
    bits = [jnp.where((me & 1) == 0, (me >> orders[0][t]) & 1, (me >> orders[1][t]) & 1) for t in range(steps)]
    cur = keep + lax.ppermute(send, "rows", _pairs(size, orders, 0))
    for t in range(1, steps):
        half = cur.shape[axis] // 2
        lo = lax.slice_in_dim(cur, 0, half, axis=axis)
        hi = lax.slice_in_dim(cur, half, 2 * half, axis=axis)
        low = bits[t] == 0
        keep = jnp.where(low, lo, hi)
        send = jnp.where(low, hi, lo)
        cur = keep + lax.ppermute(send, "rows", _pairs(size, orders, t))
    for t in reversed(range(steps)):
        low = bits[t] == 0
        cur = _join(cur, lax.ppermute(cur, "rows", _pairs(size, orders, t)), low, axis)
    return cur


def _allgather(x, size):
    me = lax.axis_index("rows")
    cur = x
    for s in reversed(range(_steps(size))):
        low = ((me >> s) & 1) == 0
        other = lax.ppermute(cur, "rows", _xor_pairs(size, s))
        cur = jnp.where(low, jnp.stack([cur, other], -2), jnp.stack([other, cur], -2))
    return cur.reshape(*x.shape[:-1], size * x.shape[-1])


def _bf16_round(x):
    return lax.reduce_precision(x, exponent_bits=8, mantissa_bits=7)


def _butterfly_sum(x, size):
    for s in range(_steps(size)):
        x = x + lax.ppermute(x, "rows", _xor_pairs(size, s))
    return x


def _sums_kernel(len_ref, valid_ref, acts_ref, gout_ref, pin_ref, pout_ref, keep_ref, send_ref, act_scr, grad_scr):
    tokens, modules, width_in = acts_ref.shape
    queries = len_ref.shape[1]
    rank = pin_ref.shape[1] // modules
    width = rank * rank
    half = width // 2
    me = lax.axis_index("rows")
    act_scr[...] = jnp.dot(
        acts_ref[...].reshape(tokens * modules, width_in), pin_ref[...],
        preferred_element_type=jnp.float32,
    )
    grad_scr[...] = jnp.dot(
        gout_ref[...].reshape(tokens * modules, width_in), pout_ref[...],
        preferred_element_type=jnp.float32,
    )
    qrow = lax.broadcasted_iota(jnp.int32, (queries, queries), 0)
    qcol = lax.broadcasted_iota(jnp.int32, (queries, queries), 1)
    lengths = jnp.broadcast_to(len_ref[...], (queries, queries))
    ends = jnp.sum(jnp.where(qcol <= qrow, lengths, 0), axis=1, keepdims=True)
    pos = lax.broadcasted_iota(jnp.int32, (queries, tokens), 1) + me * tokens
    segment = jnp.sum((ends <= pos).astype(jnp.int32), axis=0, keepdims=True)
    qid = lax.broadcasted_iota(jnp.int32, (queries, tokens), 0)
    sel = ((segment == qid) & (valid_ref[...] == 1)).astype(jnp.bfloat16)
    col = lax.broadcasted_iota(jnp.int32, (modules * rank, width), 1)
    row = lax.broadcasted_iota(jnp.int32, (modules * rank, width), 0)
    first = (me % 2) == 0
    for m in range(modules):
        repeat = (m * rank + col // rank == row).astype(jnp.bfloat16)
        tile = (m * rank + col % rank == row).astype(jnp.bfloat16)
        rows = pl.ds(m, tokens, stride=modules)
        act_proj = act_scr[rows, :].astype(jnp.bfloat16)
        grad_proj = grad_scr[rows, :].astype(jnp.bfloat16)
        act_wide = jnp.dot(act_proj, tile, preferred_element_type=jnp.float32)
        grad_wide = jnp.dot(grad_proj, repeat, preferred_element_type=jnp.float32)
        outer = grad_wide * act_wide
        high = outer.astype(jnp.bfloat16)
        low = (outer - high.astype(jnp.float32)).astype(jnp.bfloat16)
        total = jnp.dot(sel, high, preferred_element_type=jnp.float32) + jnp.dot(
            sel, low, preferred_element_type=jnp.float32
        )
        lo, hi = total[:, :half], total[:, half:]
        keep_ref[m] = jnp.where(first, lo, hi)
        send_ref[m] = jnp.where(first, hi, lo)


def _module_sums(lengths, valid, acts, grads_out, proj_in, proj_out):
    queries = lengths.shape[0]
    tokens, modules, _ = acts.shape
    rank = proj_in.shape[1] // modules
    scratch = pltpu.VMEM((tokens * modules, modules * rank), jnp.float32)
    half = jax.ShapeDtypeStruct((modules, queries, rank * rank // 2), jnp.float32)
    return pl.pallas_call(
        _sums_kernel,
        out_shape=(half, half),
        scratch_shapes=[scratch, scratch],
    )(lengths.reshape(1, queries), valid.reshape(1, tokens), acts, grads_out, proj_in, proj_out)


def _split_bf16(x):
    high = x.astype(jnp.bfloat16)
    return high, (x - high.astype(jnp.float32)).astype(jnp.bfloat16)


def _precond_kernel(g_ref, f_ref, out_ref):
    nt = (((1,), (1,)), ((), ()))
    f = lambda a, b: lax.dot_general(a, b, nt, preferred_element_type=jnp.float32)
    g_high, g_low = _split_bf16(g_ref[0])
    f_high, f_low = _split_bf16(f_ref[0])
    out_ref[0] = f(g_high, f_high) + (f(g_low, f_high) + f(g_high, f_low))


def _precond(grads, fisher_inv):
    modules, queries, width = grads.shape
    cols = fisher_inv.shape[1]
    return pl.pallas_call(
        _precond_kernel,
        out_shape=jax.ShapeDtypeStruct((modules, queries, cols), jnp.float32),
        grid=(modules,),
        in_specs=[
            pl.BlockSpec((1, queries, width), lambda m: (m, 0, 0)),
            pl.BlockSpec((1, cols, width), lambda m: (m, 0, 0)),
        ],
        out_specs=pl.BlockSpec((1, queries, cols), lambda m: (m, 0, 0)),
        compiler_params=pltpu.CompilerParams(vmem_limit_bytes=48 * 1024 * 1024),
    )(grads, fisher_inv)


def shards(size, acts, grads_out, lengths, valid, proj_in, proj_out, fisher_inv, database):
    tok_rows = acts.shape[0]
    modules = acts.shape[1]
    proj_rank = proj_in.shape[1] // modules
    queries = lengths.shape[0]
    flat_width = proj_rank * proj_rank
    keep, send = _module_sums(lengths, valid, acts, grads_out, proj_in, proj_out)
    summed = _allreduce(keep, send, size, 2)
    precond_cols = _precond(summed, fisher_inv)
    scores = jnp.einsum(
        "mqk,nmk->qn",
        _allgather(precond_cols, size),
        database,
        precision=lax.Precision.HIGH,
    )
    db_count = database.shape[0] * size
    moments = _butterfly_sum(
        jnp.stack([jnp.sum(scores, axis=1), jnp.sum(scores * scores, axis=1)]), size
    )
    avg_score = moments[0] / db_count
    variance = moments[1] / db_count - avg_score * avg_score
    centred = scores - avg_score[:, None]
    return centred * lax.rsqrt(variance + 1e-06)[:, None]


def solution(mesh):
    size = mesh.shape["rows"]
    placed = (
        P(("groups", "rows"), None, None),
        P(("groups", "rows"), None, None),
        P("groups"),
        P(("groups", "rows")),
        P(),
        P(),
        P(None, "rows", None),
        P(("groups", "rows"), None, None),
    )
    return jax.shard_map(
        lambda *a: shards(size, *a),
        mesh=mesh,
        in_specs=placed,
        out_specs=P(None, ("groups", "rows")),
        check_vma=False,
    )
```

```python
import jax
import jax.numpy as jnp
from jax import lax
from jax.experimental import pallas as pl
from jax.experimental.pallas import tpu as pltpu
from jax.sharding import PartitionSpec as P


def _xor_pairs(size, bit):
    return [(i, i ^ (1 << bit)) for i in range(size)]


def _steps(size):
    steps = size.bit_length() - 1
    assert (1 << steps) == size
    return steps


def _join(mine, other, low, axis):
    return jnp.where(
        low, jnp.concatenate([mine, other], axis), jnp.concatenate([other, mine], axis)
    )


def _orders(size):
    steps = _steps(size)
    first = list(range(steps))
    second = list(first)
    if steps >= 3:
        second[1], second[2] = second[2], second[1]
    return first, second


def _pairs(size, orders, t):
    return [(i, i ^ (1 << orders[i & 1][t])) for i in range(size)]


def _allreduce(keep, send, size, axis):
    me = lax.axis_index("rows")
    orders = _orders(size)
    steps = _steps(size)
    bits = [jnp.where((me & 1) == 0, (me >> orders[0][t]) & 1, (me >> orders[1][t]) & 1) for t in range(steps)]
    recv = lax.ppermute(send, "rows", _pairs(size, orders, 0))
    for t in range(1, steps):
        half = keep.shape[axis] // 2
        part = lambda a, lo_half: lax.slice_in_dim(a, 0 if lo_half else half, half if lo_half else 2 * half, axis=axis)
        lo = part(keep, True) + part(recv, True)
        hi = part(keep, False) + part(recv, False)
        low = bits[t] == 0
        keep, send = jnp.where(low, lo, hi), jnp.where(low, hi, lo)
        recv = lax.ppermute(send, "rows", _pairs(size, orders, t))
    cur = keep + recv
    for t in reversed(range(steps)):
        low = bits[t] == 0
        cur = _join(cur, lax.ppermute(cur, "rows", _pairs(size, orders, t)), low, axis)
    return cur


def _allgather(x, size):
    me = lax.axis_index("rows")
    cur = x
    for s in reversed(range(_steps(size))):
        low = ((me >> s) & 1) == 0
        other = lax.ppermute(cur, "rows", _xor_pairs(size, s))
        cur = jnp.where(low, jnp.stack([cur, other], -2), jnp.stack([other, cur], -2))
    return cur.reshape(*x.shape[:-1], size * x.shape[-1])


def _bf16_round(x):
    return lax.reduce_precision(x, exponent_bits=8, mantissa_bits=7)


def _butterfly_sum(x, size):
    for s in range(_steps(size)):
        x = x + lax.ppermute(x, "rows", _xor_pairs(size, s))
    return x


def _sums_kernel(len_ref, valid_ref, acts_ref, gout_ref, pin_ref, pout_ref, keep_ref, send_ref, act_scr, grad_scr):
    tokens, modules, width_in = acts_ref.shape
    queries = len_ref.shape[1]
    rank = pin_ref.shape[1] // modules
    width = rank * rank
    half = width // 2
    me = lax.axis_index("rows")
    act_scr[...] = jnp.dot(
        acts_ref[...].reshape(tokens * modules, width_in), pin_ref[...],
        preferred_element_type=jnp.float32,
    )
    grad_scr[...] = jnp.dot(
        gout_ref[...].reshape(tokens * modules, width_in), pout_ref[...],
        preferred_element_type=jnp.float32,
    )
    qrow = lax.broadcasted_iota(jnp.int32, (queries, queries), 0)
    qcol = lax.broadcasted_iota(jnp.int32, (queries, queries), 1)
    lengths = jnp.broadcast_to(len_ref[...], (queries, queries))
    ends = jnp.sum(jnp.where(qcol <= qrow, lengths, 0), axis=1, keepdims=True)
    pos = lax.broadcasted_iota(jnp.int32, (queries, tokens), 1) + me * tokens
    segment = jnp.sum((ends <= pos).astype(jnp.int32), axis=0, keepdims=True)
    qid = lax.broadcasted_iota(jnp.int32, (queries, tokens), 0)
    sel = ((segment == qid) & (valid_ref[...] == 1)).astype(jnp.bfloat16)
    col = lax.broadcasted_iota(jnp.int32, (modules * rank, width), 1)
    row = lax.broadcasted_iota(jnp.int32, (modules * rank, width), 0)
    first = (me % 2) == 0
    for m in range(modules):
        repeat = (m * rank + col // rank == row).astype(jnp.bfloat16)
        tile = (m * rank + col % rank == row).astype(jnp.bfloat16)
        rows = pl.ds(m, tokens, stride=modules)
        act_proj = act_scr[rows, :].astype(jnp.bfloat16)
        grad_proj = grad_scr[rows, :].astype(jnp.bfloat16)
        act_wide = jnp.dot(act_proj, tile, preferred_element_type=jnp.float32)
        grad_wide = jnp.dot(grad_proj, repeat, preferred_element_type=jnp.float32)
        outer = grad_wide * act_wide
        high = outer.astype(jnp.bfloat16)
        low = (outer - high.astype(jnp.float32)).astype(jnp.bfloat16)
        total = jnp.dot(sel, high, preferred_element_type=jnp.float32) + jnp.dot(
            sel, low, preferred_element_type=jnp.float32
        )
        lo, hi = total[:, :half], total[:, half:]
        keep_ref[m] = jnp.where(first, lo, hi)
        send_ref[m] = jnp.where(first, hi, lo)


def _module_sums(lengths, valid, acts, grads_out, proj_in, proj_out):
    queries = lengths.shape[0]
    tokens, modules, _ = acts.shape
    rank = proj_in.shape[1] // modules
    scratch = pltpu.VMEM((tokens * modules, modules * rank), jnp.float32)
    half = jax.ShapeDtypeStruct((modules, queries, rank * rank // 2), jnp.float32)
    return pl.pallas_call(
        _sums_kernel,
        out_shape=(half, half),
        scratch_shapes=[scratch, scratch],
    )(lengths.reshape(1, queries), valid.reshape(1, tokens), acts, grads_out, proj_in, proj_out)


def _split_bf16(x):
    high = x.astype(jnp.bfloat16)
    return high, (x - high.astype(jnp.float32)).astype(jnp.bfloat16)


def _precond_kernel(g_ref, f_ref, out_ref):
    nt = (((1,), (1,)), ((), ()))
    f = lambda a, b: lax.dot_general(a, b, nt, preferred_element_type=jnp.float32)
    for m in range(g_ref.shape[0]):
        g_high, g_low = _split_bf16(g_ref[m])
        f_high, f_low = _split_bf16(f_ref[m])
        out_ref[m] = f(g_high, f_high) + (f(g_low, f_high) + f(g_high, f_low))


def _precond(grads, fisher_inv):
    modules, queries, _ = grads.shape
    return pl.pallas_call(
        _precond_kernel,
        out_shape=jax.ShapeDtypeStruct((modules, queries, fisher_inv.shape[1]), jnp.float32),
        compiler_params=pltpu.CompilerParams(vmem_limit_bytes=48 * 1024 * 1024),
    )(grads, fisher_inv)


def shards(size, acts, grads_out, lengths, valid, proj_in, proj_out, fisher_inv, database):
    tok_rows = acts.shape[0]
    modules = acts.shape[1]
    proj_rank = proj_in.shape[1] // modules
    queries = lengths.shape[0]
    flat_width = proj_rank * proj_rank
    keep, send = _module_sums(lengths, valid, acts, grads_out, proj_in, proj_out)
    summed = _allreduce(keep, send, size, 2)
    precond_cols = _precond(summed, fisher_inv)
    scores = jnp.einsum(
        "mqk,nmk->qn",
        _allgather(precond_cols, size),
        database,
        precision=lax.Precision.HIGH,
    )
    db_count = database.shape[0] * size
    moments = _butterfly_sum(
        jnp.stack([jnp.sum(scores, axis=1), jnp.sum(scores * scores, axis=1)]), size
    )
    avg_score = moments[0] / db_count
    variance = moments[1] / db_count - avg_score * avg_score
    centred = scores - avg_score[:, None]
    return centred * lax.rsqrt(variance + 1e-06)[:, None]


def solution(mesh):
    size = mesh.shape["rows"]
    placed = (
        P(("groups", "rows"), None, None),
        P(("groups", "rows"), None, None),
        P("groups"),
        P(("groups", "rows")),
        P(),
        P(),
        P(None, "rows", None),
        P(("groups", "rows"), None, None),
    )
    return jax.shard_map(
        lambda *a: shards(size, *a),
        mesh=mesh,
        in_specs=placed,
        out_specs=P(None, ("groups", "rows")),
        check_vma=False,
    )
```
